256 devices in a mesh: shots: 8 (over z_hi, y), slab: 32 (over z_lo, x, core).
Axes of the slice: x: 4, y: 4, z: 8 (z_hi: 2, z_lo: 4; z = z_hi * 4 + z_lo), core: 2. Of those that a mesh axis runs over, the one named last changes fastest.
Arguments:
- vel_parts: float32 [8, 128, 512, 256], P('shots', 'slab'), may hold values from -24 to 24
- den_parts: float32 [8, 128, 512, 256], P('shots', 'slab'), may hold values from -24 to 24
- illum_parts: float32 [8, 128, 512, 256], P('shots', 'slab'), may hold values from 0.02 to 0.2
- layer_index: int32 [256], replicated, may hold values from 0 to 15, never falling along the last dimension, each value on 1 to 128 neighbouring positions
- depth_scale: float32 [2, 16], replicated, may hold values from 1 to 8
Outputs:
- vel_update: float32 [128, 512, 256], P('slab')
- den_update: float32 [128, 512, 256], P('slab')
The draws below stay inside these ranges and needn't reach their ends.
Inputs may be any that keep to these rules, and one draw needn't show every extreme that they name: `layer_index`: never falls with depth; every layer holds 1 to 128 consecutive depth cells, and one holds exactly 128.
All inputs are finite; a program needn't handle non-finite values.
Results may differ from the reference program's by a relative error of at most 0.00011.
Values sent between devices are 32-bit elements; how exact they have to be, the bound alone decides.
No kernel may reach another device: no remote copies, remote signals or barrier semaphores. Data moves between devices by JAX's collectives and lax.ppermute only.
A program may use at most 64 MiB of HBM per device.

```python
import math
import jax
import jax.numpy as jnp
import numpy as np
from jax import lax

NY = 512
NZ = 256
RADIUS = 20
LAYERS = 16
NX = 128
N_SHOTS = 8


def shard_levels(stream_key, extent, shards, smallest, top_value):
    def one(axis_at, parts):
        draws = jax.random.uniform(jax.random.fold_in(jax.random.fold_in(stream_key, 6), axis_at), (parts,), jnp.float32, smallest / len(shards), top_value / len(shards))
        return jnp.repeat(jnp.exp(draws), extent[axis_at] // parts).reshape((-1,) + (1,) * (len(extent) - axis_at - 1))

    gain = one(*shards[0])
    for cut in shards[1:]:
        gain = gain * one(*cut)
    return gain


def length_profile(number_of, total, reach, skew):
    portions = [(1 << 20) // math.isqrt(grade ** skew) + 1 for grade in range(2, number_of + 1)]
    surplus, holding = total - reach - (number_of - 1), [1] * (number_of - 1)
    while surplus > 0:
        candidates = [i for i in range(number_of - 1) if holding[i] < reach]
        mass, remaining = sum([portions[i] for i in candidates]), surplus
        for i in candidates:
            extra = min(reach - holding[i], max(1, remaining * portions[i] // mass), surplus)
            holding[i] = holding[i] + extra
            surplus = surplus - extra
    return np.array([reach] + holding)


def ragged_sizes(own_key, number_of, total, limit, slope):
    if number_of == 2:
        one = jax.random.randint(own_key, (), max(1, total - limit), min(limit, total - 1) + 1)
        return jnp.stack([one, total - one])
    lengths = jnp.asarray(length_profile(number_of, total, limit, slope), jnp.int32)
    pairs = (number_of - 1) // 2
    donor, sink = lengths[1:1 + 2 * pairs:2], lengths[2:2 + 2 * pairs:2]
    slack = jnp.minimum(donor - 1, limit - sink)
    moved = jax.random.randint(jax.random.fold_in(own_key, 1), (pairs,), 0, 1 << 20) % (slack + 1)
    lengths = lengths.at[1:1 + 2 * pairs:2].set(donor - moved).at[2:2 + 2 * pairs:2].set(sink + moved)
    return lengths[jax.random.permutation(jax.random.fold_in(own_key, 2), number_of)]


def centred(stream_key, dims, deviation, limit, cuts=(), held_as=jnp.bfloat16):
    entries = jax.random.normal(stream_key, dims, jnp.float32) * deviation
    if len(cuts) > 0:
        entries = shard_levels(stream_key, dims, cuts, -0.22, 0.18) * entries
    return jnp.clip(entries, min=-limit, max=limit).astype(held_as)


def setup_inputs(seed: int = 0) -> dict:
    seeds = jax.random.split(jax.random.key(seed), 6)
    vel_parts = centred(seeds[0], (N_SHOTS, NX, NY, NZ), 4.0, 24.0, ((0, 8), (1, 32)), jnp.float32)
    den_parts = centred(seeds[1], (N_SHOTS, NX, NY, NZ), 4.0, 24.0, ((0, 8), (1, 32)), jnp.float32)
    illum_parts = jnp.clip(jnp.exp(math.log(0.2) - 2.3025851 * jax.random.uniform(seeds[2], (N_SHOTS, NX, NY, NZ), jnp.float32) ** shard_levels(seeds[2], (N_SHOTS, NX, NY, NZ), ((0, 8), (1, 32)), -0.2, 0.2)), 0.02, 0.2)
    layer_index = jnp.searchsorted(jnp.cumsum(ragged_sizes(seeds[3], LAYERS, NZ, NZ // 2, 1)), jnp.arange(NZ), side="right").astype(jnp.int32)
    depth_scale = jnp.clip(jnp.exp(jax.random.uniform(seeds[4], (2, LAYERS), jnp.float32, math.log(1.0), math.log(8.0))), 1.0, 8.0)
    return {"vel_parts": vel_parts, "den_parts": den_parts, "illum_parts": illum_parts, "layer_index": layer_index, "depth_scale": depth_scale}


def smoothing_matrix(count):
    cells = jnp.arange(count, dtype=jnp.int32)
    offset = (cells[:, None] - cells[None, :]).astype(jnp.float32)
    inside = jnp.abs(offset) <= RADIUS
    weights = jnp.where(inside, jnp.exp(-offset * offset / 200.0), jnp.float32(0.0))
    return weights / jnp.sum(weights, axis=1, keepdims=True)


def smooth_all(field):
    hp = lax.Precision.HIGHEST
    field = jnp.einsum("ij,jyz->iyz", smoothing_matrix(field.shape[0]), field, precision=hp)
    field = jnp.einsum("ij,xjz->xiz", smoothing_matrix(field.shape[1]), field, precision=hp)
    field = jnp.einsum("xyj,ij->xyi", field, smoothing_matrix(field.shape[2]), precision=hp)
    return field


def reference(vel_parts, den_parts, illum_parts, layer_index, depth_scale):
    vel = jnp.sum(vel_parts, axis=0)
    den = jnp.sum(den_parts, axis=0)
    illum = jnp.sum(illum_parts, axis=0)
    vel_pre = vel / illum
    den_pre = den / illum
    onehot = (layer_index[:, None] == jnp.arange(LAYERS, dtype=jnp.int32)[None, :]).astype(jnp.float32)
    per_depth = jnp.dot(depth_scale, onehot.T, precision=lax.Precision.HIGHEST)
    vel_update = per_depth[0][None, None, :] * smooth_all(vel_pre)
    den_update = per_depth[1][None, None, :] * smooth_all(den_pre)
    return vel_update, den_update
```

```python
import jax
import jax.numpy as jnp
from jax import lax
from jax.sharding import PartitionSpec as P

RADIUS = 20
HP = lax.Precision.HIGHEST


def smoothing_matrix(count):
    cells = jnp.arange(count, dtype=jnp.int32)
    offset = (cells[:, None] - cells[None, :]).astype(jnp.float32)
    inside = jnp.abs(offset) <= RADIUS
    weights = jnp.where(inside, jnp.exp(-offset * offset / 200.0), jnp.float32(0.0))
    return weights / jnp.sum(weights, axis=1, keepdims=True)


def smooth_depth(field):
    matrix = smoothing_matrix(field.shape[2])
    return jnp.einsum("xyj,ij->xyi", field, matrix, precision=HP)


def smooth_across(field):
    matrix = smoothing_matrix(field.shape[1])
    return jnp.einsum("ij,xjz->xiz", matrix, field, precision=HP)


def smooth_along_x(field):
    cols = lax.all_to_all(field, "slab", split_axis=1, concat_axis=0, tiled=True)
    matrix = smoothing_matrix(cols.shape[0])
    cols = jnp.einsum("ij,jyz->iyz", matrix, cols, precision=HP)
    return lax.all_to_all(cols, "slab", split_axis=0, concat_axis=1, tiled=True)


def body(vel_parts, den_parts, illum_parts, layer_index, depth_scale):
    vel, den, illum = lax.psum_scatter(
        (vel_parts[0], den_parts[0], illum_parts[0]), "shots", scatter_dimension=1, tiled=True
    )
    vel = smooth_along_x(smooth_depth(vel / illum))
    den = smooth_along_x(smooth_depth(den / illum))
    vel, den = lax.all_gather((vel, den), "shots", axis=1, tiled=True)
    vel = smooth_across(vel)
    den = smooth_across(den)
    onehot = (
        layer_index[:, None] == jnp.arange(depth_scale.shape[1], dtype=jnp.int32)[None, :]
    ).astype(jnp.float32)
    per_depth = jnp.dot(depth_scale, onehot.T, precision=HP)
    vel_update = per_depth[0][None, None, :] * vel
    den_update = per_depth[1][None, None, :] * den
    return (vel_update, den_update)


def solution(mesh):
    placed = (
        P("shots", "slab", None, None),
        P("shots", "slab", None, None),
        P("shots", "slab", None, None),
        P(),
        P(),
    )
    return jax.shard_map(
        body,
        mesh=mesh,
        in_specs=placed,
        out_specs=(P("slab", None, None), P("slab", None, None)),
        check_vma=False,
    )
```

```python
import jax
import jax.numpy as jnp
from jax import lax
from jax.sharding import PartitionSpec as P

RADIUS = 20
HP = lax.Precision.HIGHEST
RING = 4


def smoothing_matrix(count):
    cells = jnp.arange(count, dtype=jnp.int32)
    offset = (cells[:, None] - cells[None, :]).astype(jnp.float32)
    inside = jnp.abs(offset) <= RADIUS
    weights = jnp.where(inside, jnp.exp(-offset * offset / 200.0), jnp.float32(0.0))
    return weights / jnp.sum(weights, axis=1, keepdims=True)


def ring_pairs(n_shots, step):
    hi = n_shots // RING
    return [(h * RING + r, h * RING + (r + step) % RING) for h in range(hi) for r in range(RING)]


def hi_pairs(n_shots):
    hi = n_shots // RING
    return [(h * RING + r, ((h + 1) % hi) * RING + r) for h in range(hi) for r in range(RING)]


def rows(field, start, size):
    return lax.dynamic_slice_in_dim(field, start, size, axis=1)


def reduce_scatter_shots(fields, n_shots):
    idx = lax.axis_index("shots")
    r, h = idx % RING, idx // RING
    chunk = fields[0].shape[1] // RING
    half = chunk // 2
    fwd, bwd = ring_pairs(n_shots, 1), ring_pairs(n_shots, -1)
    acc_f = [rows(f, ((r - 1) % RING) * chunk + h * half, half) for f in fields]
    acc_b = [rows(f, ((r + 1) % RING) * chunk + (1 - h) * half, half) for f in fields]
    for t in range(1, RING):
        recv_f = lax.ppermute(acc_f, "shots", fwd)
        recv_b = lax.ppermute(acc_b, "shots", bwd)
        acc_f = [x + rows(f, ((r - 1 - t) % RING) * chunk + h * half, half) for x, f in zip(recv_f, fields)]
        acc_b = [x + rows(f, ((r + 1 + t) % RING) * chunk + (1 - h) * half, half) for x, f in zip(recv_b, fields)]
    other = lax.ppermute(acc_b, "shots", hi_pairs(n_shots))
    return [a + b for a, b in zip(acc_f, other)]


def all_gather_shots(blocks, n_shots, total):
    idx = lax.axis_index("shots")
    r, h = idx % RING, idx // RING
    chunk = total // RING
    half = chunk // 2
    fwd, bwd = ring_pairs(n_shots, 1), ring_pairs(n_shots, -1)
    outs = [jnp.zeros(b.shape[:1] + (total,) + b.shape[2:], b.dtype) for b in blocks]

    def place(outs, pieces, start):
        return [lax.dynamic_update_slice_in_dim(o, p, start, axis=1) for o, p in zip(outs, pieces)]

    cur_f = list(blocks)
    cur_b = lax.ppermute(cur_f, "shots", hi_pairs(n_shots))
    outs = place(outs, cur_f, r * chunk + h * half)
    outs = place(outs, cur_b, r * chunk + (1 - h) * half)
    for t in range(1, RING):
        cur_f = lax.ppermute(cur_f, "shots", fwd)
        cur_b = lax.ppermute(cur_b, "shots", bwd)
        outs = place(outs, cur_f, ((r - t) % RING) * chunk + h * half)
        outs = place(outs, cur_b, ((r + t) % RING) * chunk + (1 - h) * half)
    return outs


def smooth_depth(field):
    matrix = smoothing_matrix(field.shape[-1])
    return jnp.einsum("...j,ij->...i", field, matrix, precision=HP)


def smooth_across(field):
    matrix = smoothing_matrix(field.shape[1])
    return jnp.einsum("ij,xjz->xiz", matrix, field, precision=HP)


def smooth_along_x(both):
    cols = lax.all_to_all(both, "slab", split_axis=2, concat_axis=1, tiled=True)
    matrix = smoothing_matrix(cols.shape[1])
    cols = jnp.einsum("ij,fjyz->fiyz", matrix, cols, precision=HP)
    return lax.all_to_all(cols, "slab", split_axis=1, concat_axis=2, tiled=True)


def make_body(n_shots):
    def body(vel_parts, den_parts, illum_parts, layer_index, depth_scale):
        total = vel_parts.shape[2]
        vel, den, illum = reduce_scatter_shots(
            [vel_parts[0], den_parts[0], illum_parts[0]], n_shots
        )
        both = jnp.stack([vel / illum, den / illum])
        both = smooth_along_x(smooth_depth(both))
        vel, den = all_gather_shots([both[0], both[1]], n_shots, total)
        vel = smooth_across(vel)
        den = smooth_across(den)
        onehot = (
            layer_index[:, None] == jnp.arange(depth_scale.shape[1], dtype=jnp.int32)[None, :]
        ).astype(jnp.float32)
        per_depth = jnp.dot(depth_scale, onehot.T, precision=HP)
        vel_update = per_depth[0][None, None, :] * vel
        den_update = per_depth[1][None, None, :] * den
        return (vel_update, den_update)

    return body


def solution(mesh):
    placed = (
        P("shots", "slab", None, None),
        P("shots", "slab", None, None),
        P("shots", "slab", None, None),
        P(),
        P(),
    )
    return jax.shard_map(
        make_body(mesh.shape["shots"]),
        mesh=mesh,
        in_specs=placed,
        out_specs=(P("slab", None, None), P("slab", None, None)),
        check_vma=False,
    )
```

```python
import jax
import jax.numpy as jnp
from jax import lax
from jax.sharding import PartitionSpec as P

RADIUS = 20
HP = lax.Precision.HIGHEST
RING = 4


def smoothing_matrix(count):
    cells = jnp.arange(count, dtype=jnp.int32)
    offset = (cells[:, None] - cells[None, :]).astype(jnp.float32)
    inside = jnp.abs(offset) <= RADIUS
    weights = jnp.where(inside, jnp.exp(-offset * offset / 200.0), jnp.float32(0.0))
    return weights / jnp.sum(weights, axis=1, keepdims=True)


def ring_pairs(n_shots, step):
    hi = n_shots // RING
    return [(h * RING + r, h * RING + (r + step) % RING) for h in range(hi) for r in range(RING)]


def hi_pairs(n_shots):
    hi = n_shots // RING
    return [(h * RING + r, ((h + 1) % hi) * RING + r) for h in range(hi) for r in range(RING)]


def rows(field, start, size):
    return lax.dynamic_slice_in_dim(field, start, size, axis=1)


def reduce_scatter_shots(fields, n_shots):
    idx = lax.axis_index("shots")
    r, h = idx % RING, idx // RING
    chunk = fields[0].shape[1] // RING
    half = chunk // 2
    fwd, bwd = ring_pairs(n_shots, 1), ring_pairs(n_shots, -1)
    acc_f = [rows(f, ((r - 1) % RING) * chunk + h * half, half) for f in fields]
    acc_b = [rows(f, ((r + 1) % RING) * chunk + (1 - h) * half, half) for f in fields]
    for t in range(1, RING):
        recv_f = lax.ppermute(acc_f, "shots", fwd)
        recv_b = lax.ppermute(acc_b, "shots", bwd)
        acc_f = [x + rows(f, ((r - 1 - t) % RING) * chunk + h * half, half) for x, f in zip(recv_f, fields)]
        acc_b = [x + rows(f, ((r + 1 + t) % RING) * chunk + (1 - h) * half, half) for x, f in zip(recv_b, fields)]
    other = lax.ppermute(acc_b, "shots", hi_pairs(n_shots))
    return [a + b for a, b in zip(acc_f, other)]


def all_gather_smooth_shots(blocks, n_shots, total):
    idx = lax.axis_index("shots")
    r, h = idx % RING, idx // RING
    chunk = total // RING
    half = chunk // 2
    fwd, bwd = ring_pairs(n_shots, 1), ring_pairs(n_shots, -1)
    cur_f = list(blocks)
    cur_b = lax.ppermute(cur_f, "shots", hi_pairs(n_shots))
    pieces = [cur_f, cur_b]
    starts = [r * chunk + h * half, r * chunk + (1 - h) * half]
    for t in range(1, RING):
        cur_f = lax.ppermute(cur_f, "shots", fwd)
        cur_b = lax.ppermute(cur_b, "shots", bwd)
        pieces += [cur_f, cur_b]
        starts += [((r - t) % RING) * chunk + h * half, ((r + t) % RING) * chunk + (1 - h) * half]
    matrix = smoothing_matrix(total)
    matrix = jnp.concatenate(
        [lax.dynamic_slice_in_dim(matrix, s, half, axis=1) for s in starts], axis=1
    )
    outs = []
    for k in range(len(blocks)):
        joined = jnp.concatenate([p[k] for p in pieces], axis=1)
        wide = jnp.broadcast_to(matrix, (joined.shape[0],) + matrix.shape)
        outs.append(jnp.einsum("xij,xjz->xiz", wide, joined, precision=HP))
    return outs


def smooth_depth(field):
    matrix = smoothing_matrix(field.shape[-1])
    return jnp.einsum("...j,ij->...i", field, matrix, precision=HP)


def smooth_along_x(both):
    cols = lax.all_to_all(both, "slab", split_axis=2, concat_axis=1, tiled=True)
    matrix = smoothing_matrix(cols.shape[1])
    cols = jnp.einsum("ij,fjyz->fiyz", matrix, cols, precision=HP)
    return lax.all_to_all(cols, "slab", split_axis=1, concat_axis=2, tiled=True)


def make_body(n_shots):
    def body(vel_parts, den_parts, illum_parts, layer_index, depth_scale):
        total = vel_parts.shape[2]
        vel, den, illum = reduce_scatter_shots(
            [vel_parts[0], den_parts[0], illum_parts[0]], n_shots
        )
        both = jnp.stack([vel / illum, den / illum])
        both = smooth_along_x(smooth_depth(both))
        vel, den = all_gather_smooth_shots([both[0], both[1]], n_shots, total)
        onehot = (
            layer_index[:, None] == jnp.arange(depth_scale.shape[1], dtype=jnp.int32)[None, :]
        ).astype(jnp.float32)
        per_depth = jnp.dot(depth_scale, onehot.T, precision=HP)
        vel_update = per_depth[0][None, None, :] * vel
        den_update = per_depth[1][None, None, :] * den
        return (vel_update, den_update)

    return body


def solution(mesh):
    placed = (
        P("shots", "slab", None, None),
        P("shots", "slab", None, None),
        P("shots", "slab", None, None),
        P(),
        P(),
    )
    return jax.shard_map(
        make_body(mesh.shape["shots"]),
        mesh=mesh,
        in_specs=placed,
        out_specs=(P("slab", None, None), P("slab", None, None)),
        check_vma=False,
    )
```

```python
import jax
import jax.numpy as jnp
from jax import lax
from jax.sharding import PartitionSpec as P

RADIUS = 20
HP = lax.Precision.HIGHEST
RING = 4


def smoothing_matrix(count):
    cells = jnp.arange(count, dtype=jnp.int32)
    offset = (cells[:, None] - cells[None, :]).astype(jnp.float32)
    inside = jnp.abs(offset) <= RADIUS
    weights = jnp.where(inside, jnp.exp(-offset * offset / 200.0), jnp.float32(0.0))
    return weights / jnp.sum(weights, axis=1, keepdims=True)


def ring_pairs(n_shots, step):
    hi = n_shots // RING
    return [(h * RING + r, h * RING + (r + step) % RING) for h in range(hi) for r in range(RING)]


def hi_pairs(n_shots):
    hi = n_shots // RING
    return [(h * RING + r, ((h + 1) % hi) * RING + r) for h in range(hi) for r in range(RING)]


def rows(field, start, size):
    return lax.dynamic_slice_in_dim(field, start, size, axis=1)


def reduce_scatter_shots(fields, n_shots):
    idx = lax.axis_index("shots")
    r, h = idx % RING, idx // RING
    chunk = fields[0].shape[1] // RING
    half = chunk // 2
    fwd, bwd = ring_pairs(n_shots, 1), ring_pairs(n_shots, -1)
    acc_f = [rows(f, ((r - 1) % RING) * chunk + h * half, half) for f in fields]
    acc_b = [rows(f, ((r + 1) % RING) * chunk + (1 - h) * half, half) for f in fields]
    for t in range(1, RING):
        recv_f = lax.ppermute(acc_f, "shots", fwd)
        recv_b = lax.ppermute(acc_b, "shots", bwd)
        acc_f = [x + rows(f, ((r - 1 - t) % RING) * chunk + h * half, half) for x, f in zip(recv_f, fields)]
        acc_b = [x + rows(f, ((r + 1 + t) % RING) * chunk + (1 - h) * half, half) for x, f in zip(recv_b, fields)]
    other = lax.ppermute(acc_b, "shots", hi_pairs(n_shots))
    return [a + b for a, b in zip(acc_f, other)]


def all_gather_smooth_shots(blocks, n_shots, total):
    idx = lax.axis_index("shots")
    r, h = idx % RING, idx // RING
    chunk = total // RING
    half = chunk // 2
    fwd, bwd = ring_pairs(n_shots, 1), ring_pairs(n_shots, -1)
    cur_f = list(blocks)
    cur_b = lax.ppermute(cur_f, "shots", hi_pairs(n_shots))
    pieces = [cur_f, cur_b]
    starts = [r * chunk + h * half, r * chunk + (1 - h) * half]
    for t in range(1, RING):
        cur_f = lax.ppermute(cur_f, "shots", fwd)
        cur_b = lax.ppermute(cur_b, "shots", bwd)
        pieces += [cur_f, cur_b]
        starts += [((r - t) % RING) * chunk + h * half, ((r + t) % RING) * chunk + (1 - h) * half]
    matrix = smoothing_matrix(total)
    matrix = jnp.concatenate(
        [lax.dynamic_slice_in_dim(matrix, s, half, axis=1) for s in starts], axis=1
    )
    outs = []
    for k in range(len(blocks)):
        joined = jnp.concatenate([p[k] for p in pieces], axis=1)
        wide = jnp.broadcast_to(matrix, (joined.shape[0],) + matrix.shape)
        outs.append(jnp.einsum("xij,xjz->xiz", wide, joined, precision=HP))
    return outs


def smooth_depth(field):
    matrix = smoothing_matrix(field.shape[-1])
    return jnp.einsum("...j,ij->...i", field, matrix, precision=HP)


def smooth_along_x(field):
    cols = lax.all_to_all(field, "slab", split_axis=1, concat_axis=0, tiled=True)
    matrix = smoothing_matrix(cols.shape[0])
    cols = jnp.einsum("ij,jyz->iyz", matrix, cols, precision=HP)
    return lax.all_to_all(cols, "slab", split_axis=0, concat_axis=1, tiled=True)


def make_body(n_shots):
    def body(vel_parts, den_parts, illum_parts, layer_index, depth_scale):
        total = vel_parts.shape[2]
        illum, vel = reduce_scatter_shots([illum_parts[0], vel_parts[0]], n_shots)
        den_mine, illum, vel = lax.optimization_barrier((den_parts[0], illum, vel))
        (den,) = reduce_scatter_shots([den_mine], n_shots)
        (vel,) = all_gather_smooth_shots([smooth_along_x(smooth_depth(vel / illum))], n_shots, total)
        (den,) = all_gather_smooth_shots([smooth_along_x(smooth_depth(den / illum))], n_shots, total)
        onehot = (
            layer_index[:, None] == jnp.arange(depth_scale.shape[1], dtype=jnp.int32)[None, :]
        ).astype(jnp.float32)
        per_depth = jnp.dot(depth_scale, onehot.T, precision=HP)
        vel_update = per_depth[0][None, None, :] * vel
        den_update = per_depth[1][None, None, :] * den
        return (vel_update, den_update)

    return body


def solution(mesh):
    placed = (
        P("shots", "slab", None, None),
        P("shots", "slab", None, None),
        P("shots", "slab", None, None),
        P(),
        P(),
    )
    return jax.shard_map(
        make_body(mesh.shape["shots"]),
        mesh=mesh,
        in_specs=placed,
        out_specs=(P("slab", None, None), P("slab", None, None)),
        check_vma=False,
    )
```

```python
import jax
import jax.numpy as jnp
from jax import lax
from jax.sharding import PartitionSpec as P

RADIUS = 20
HP = lax.Precision.HIGHEST
RING = 4


def smoothing_matrix(count):
    cells = jnp.arange(count, dtype=jnp.int32)
    offset = (cells[:, None] - cells[None, :]).astype(jnp.float32)
    inside = jnp.abs(offset) <= RADIUS
    weights = jnp.where(inside, jnp.exp(-offset * offset / 200.0), jnp.float32(0.0))
    return weights / jnp.sum(weights, axis=1, keepdims=True)


def ring_pairs(n_shots, step):
    hi = n_shots // RING
    return [(h * RING + r, h * RING + (r + step) % RING) for h in range(hi) for r in range(RING)]


def hi_pairs(n_shots):
    hi = n_shots // RING
    return [(h * RING + r, ((h + 1) % hi) * RING + r) for h in range(hi) for r in range(RING)]


def rows(field, start, size):
    return lax.dynamic_slice_in_dim(field, start, size, axis=1)


def reduce_scatter_shots(fields, n_shots):
    idx = lax.axis_index("shots")
    r, h = idx % RING, idx // RING
    chunk = fields[0].shape[1] // RING
    half = chunk // 2
    fwd, bwd = ring_pairs(n_shots, 1), ring_pairs(n_shots, -1)
    acc_f = [rows(f, ((r - 1) % RING) * chunk + h * half, half) for f in fields]
    acc_b = [rows(f, ((r + 1) % RING) * chunk + (1 - h) * half, half) for f in fields]
    for t in range(1, RING):
        recv_f = lax.ppermute(acc_f, "shots", fwd)
        recv_b = lax.ppermute(acc_b, "shots", bwd)
        acc_f = [x + rows(f, ((r - 1 - t) % RING) * chunk + h * half, half) for x, f in zip(recv_f, fields)]
        acc_b = [x + rows(f, ((r + 1 + t) % RING) * chunk + (1 - h) * half, half) for x, f in zip(recv_b, fields)]
    other = lax.ppermute(acc_b, "shots", hi_pairs(n_shots))
    return [a + b for a, b in zip(acc_f, other)]


def reduce_scatter_shots_hi_first(fields, n_shots):
    idx = lax.axis_index("shots")
    r, h = idx % RING, idx // RING
    chunk = fields[0].shape[1] // RING
    half = chunk // 2
    quarter = half // 2
    fwd, bwd = ring_pairs(n_shots, 1), ring_pairs(n_shots, -1)
    mine = [[rows(f, c * chunk + h * half, half) for c in range(RING)] for f in fields]
    theirs = [[rows(f, c * chunk + (1 - h) * half, half) for c in range(RING)] for f in fields]
    got = lax.ppermute(theirs, "shots", hi_pairs(n_shots))
    joined = [
        jnp.concatenate([a + b for a, b in zip(m, g)], axis=1) for m, g in zip(mine, got)
    ]
    acc_f = [rows(j, ((r - 1) % RING) * half, quarter) for j in joined]
    acc_b = [rows(j, ((r + 1) % RING) * half + quarter, quarter) for j in joined]
    for t in range(1, RING):
        recv_f = lax.ppermute(acc_f, "shots", fwd)
        recv_b = lax.ppermute(acc_b, "shots", bwd)
        acc_f = [x + rows(j, ((r - 1 - t) % RING) * half, quarter) for x, j in zip(recv_f, joined)]
        acc_b = [x + rows(j, ((r + 1 + t) % RING) * half + quarter, quarter) for x, j in zip(recv_b, joined)]
    return [jnp.concatenate([a, b], axis=1) for a, b in zip(acc_f, acc_b)]


def all_gather_smooth_shots(blocks, n_shots, total):
    idx = lax.axis_index("shots")
    r, h = idx % RING, idx // RING
    chunk = total // RING
    half = chunk // 2
    fwd, bwd = ring_pairs(n_shots, 1), ring_pairs(n_shots, -1)
    cur_f = list(blocks)
    cur_b = lax.ppermute(cur_f, "shots", hi_pairs(n_shots))
    pieces = [cur_f, cur_b]
    starts = [r * chunk + h * half, r * chunk + (1 - h) * half]
    for t in range(1, RING):
        cur_f = lax.ppermute(cur_f, "shots", fwd)
        cur_b = lax.ppermute(cur_b, "shots", bwd)
        pieces += [cur_f, cur_b]
        starts += [((r - t) % RING) * chunk + h * half, ((r + t) % RING) * chunk + (1 - h) * half]
    matrix = smoothing_matrix(total)
    matrix = jnp.concatenate(
        [lax.dynamic_slice_in_dim(matrix, s, half, axis=1) for s in starts], axis=1
    )
    outs = []
    for k in range(len(blocks)):
        joined = jnp.concatenate([p[k] for p in pieces], axis=1)
        wide = jnp.broadcast_to(matrix, (joined.shape[0],) + matrix.shape)
        outs.append(jnp.einsum("xij,xjz->xiz", wide, joined, precision=HP))
    return outs


def smooth_depth(field):
    matrix = smoothing_matrix(field.shape[-1])
    return jnp.einsum("...j,ij->...i", field, matrix, precision=HP)


def smooth_along_x(both):
    cols = lax.all_to_all(both, "slab", split_axis=2, concat_axis=1, tiled=True)
    matrix = smoothing_matrix(cols.shape[1])
    cols = jnp.einsum("ij,fjyz->fiyz", matrix, cols, precision=HP)
    return lax.all_to_all(cols, "slab", split_axis=1, concat_axis=2, tiled=True)


def make_body(n_shots):
    def body(vel_parts, den_parts, illum_parts, layer_index, depth_scale):
        total = vel_parts.shape[2]
        illum, vel = reduce_scatter_shots([illum_parts[0], vel_parts[0]], n_shots)
        (den,) = reduce_scatter_shots_hi_first([den_parts[0]], n_shots)
        both = jnp.stack([vel / illum, den / illum])
        both = smooth_along_x(smooth_depth(both))
        vel, den = all_gather_smooth_shots([both[0], both[1]], n_shots, total)
        onehot = (
            layer_index[:, None] == jnp.arange(depth_scale.shape[1], dtype=jnp.int32)[None, :]
        ).astype(jnp.float32)
        per_depth = jnp.dot(depth_scale, onehot.T, precision=HP)
        vel_update = per_depth[0][None, None, :] * vel
        den_update = per_depth[1][None, None, :] * den
        return (vel_update, den_update)

    return body


def solution(mesh):
    placed = (
        P("shots", "slab", None, None),
        P("shots", "slab", None, None),
        P("shots", "slab", None, None),
        P(),
        P(),
    )
    return jax.shard_map(
        make_body(mesh.shape["shots"]),
        mesh=mesh,
        in_specs=placed,
        out_specs=(P("slab", None, None), P("slab", None, None)),
        check_vma=False,
    )
```

```python
import jax
import jax.numpy as jnp
from jax import lax
from jax.sharding import PartitionSpec as P

RADIUS = 20
HP = lax.Precision.HIGHEST
RING = 4


def smoothing_matrix(count):
    cells = jnp.arange(count, dtype=jnp.int32)
    offset = (cells[:, None] - cells[None, :]).astype(jnp.float32)
    inside = jnp.abs(offset) <= RADIUS
    weights = jnp.where(inside, jnp.exp(-offset * offset / 200.0), jnp.float32(0.0))
    return weights / jnp.sum(weights, axis=1, keepdims=True)


def ring_pairs(n_shots, step):
    hi = n_shots // RING
    return [(h * RING + r, h * RING + (r + step) % RING) for h in range(hi) for r in range(RING)]


def hi_pairs(n_shots):
    hi = n_shots // RING
    return [(h * RING + r, ((h + 1) % hi) * RING + r) for h in range(hi) for r in range(RING)]


def rows(field, start, size):
    return lax.dynamic_slice_in_dim(field, start, size, axis=1)


def reduce_scatter_shots(fields, n_shots):
    idx = lax.axis_index("shots")
    r, h = idx % RING, idx // RING
    chunk = fields[0].shape[1] // RING
    half = chunk // 2
    fwd, bwd = ring_pairs(n_shots, 1), ring_pairs(n_shots, -1)

    def take(start):
        return jnp.stack([rows(f, start, half) for f in fields])

    acc_f = take(((r - 1) % RING) * chunk + h * half)
    acc_b = take(((r + 1) % RING) * chunk + (1 - h) * half)
    for t in range(1, RING):
        recv_f = lax.ppermute(acc_f, "shots", fwd)
        recv_b = lax.ppermute(acc_b, "shots", bwd)
        acc_f = recv_f + take(((r - 1 - t) % RING) * chunk + h * half)
        acc_b = recv_b + take(((r + 1 + t) % RING) * chunk + (1 - h) * half)
    return acc_f + lax.ppermute(acc_b, "shots", hi_pairs(n_shots))


def all_gather_smooth_shots(blocks, n_shots, total):
    idx = lax.axis_index("shots")
    r, h = idx % RING, idx // RING
    chunk = total // RING
    half = chunk // 2
    fwd, bwd = ring_pairs(n_shots, 1), ring_pairs(n_shots, -1)
    cur_f = blocks
    cur_b = lax.ppermute(cur_f, "shots", hi_pairs(n_shots))
    pieces = [cur_f, cur_b]
    starts = [r * chunk + h * half, r * chunk + (1 - h) * half]
    for t in range(1, RING):
        cur_f = lax.ppermute(cur_f, "shots", fwd)
        cur_b = lax.ppermute(cur_b, "shots", bwd)
        pieces += [cur_f, cur_b]
        starts += [((r - t) % RING) * chunk + h * half, ((r + t) % RING) * chunk + (1 - h) * half]
    matrix = smoothing_matrix(total)
    matrix = jnp.concatenate(
        [lax.dynamic_slice_in_dim(matrix, s, half, axis=1) for s in starts], axis=1
    )
    outs = []
    for k in range(blocks.shape[0]):
        joined = jnp.concatenate([p[k] for p in pieces], axis=1)
        wide = jnp.broadcast_to(matrix, (joined.shape[0],) + matrix.shape)
        outs.append(jnp.einsum("xij,xjz->xiz", wide, joined, precision=HP))
    return outs


def smooth_depth(field):
    matrix = smoothing_matrix(field.shape[-1])
    return jnp.einsum("...j,ij->...i", field, matrix, precision=HP)


def smooth_along_x(both):
    cols = lax.all_to_all(both, "slab", split_axis=2, concat_axis=1, tiled=True)
    matrix = smoothing_matrix(cols.shape[1])
    cols = jnp.einsum("ij,fjyz->fiyz", matrix, cols, precision=HP)
    return lax.all_to_all(cols, "slab", split_axis=1, concat_axis=2, tiled=True)


def make_body(n_shots):
    def body(vel_parts, den_parts, illum_parts, layer_index, depth_scale):
        total = vel_parts.shape[2]
        illum, vel, den = reduce_scatter_shots(
            [illum_parts[0], vel_parts[0], den_parts[0]], n_shots
        )
        both = jnp.stack([vel / illum, den / illum])
        both = smooth_along_x(smooth_depth(both))
        vel, den = all_gather_smooth_shots(both, n_shots, total)
        onehot = (
            layer_index[:, None] == jnp.arange(depth_scale.shape[1], dtype=jnp.int32)[None, :]
        ).astype(jnp.float32)
        per_depth = jnp.dot(depth_scale, onehot.T, precision=HP)
        vel_update = per_depth[0][None, None, :] * vel
        den_update = per_depth[1][None, None, :] * den
        return (vel_update, den_update)

    return body


def solution(mesh):
    placed = (
        P("shots", "slab", None, None),
        P("shots", "slab", None, None),
        P("shots", "slab", None, None),
        P(),
        P(),
    )
    return jax.shard_map(
        make_body(mesh.shape["shots"]),
        mesh=mesh,
        in_specs=placed,
        out_specs=(P("slab", None, None), P("slab", None, None)),
        check_vma=False,
    )
```

```python
import jax
import jax.numpy as jnp
from jax import lax
from jax.sharding import PartitionSpec as P

RADIUS = 20
HP = lax.Precision.HIGHEST
RING = 4


def smoothing_matrix(count):
    cells = jnp.arange(count, dtype=jnp.int32)
    offset = (cells[:, None] - cells[None, :]).astype(jnp.float32)
    inside = jnp.abs(offset) <= RADIUS
    weights = jnp.where(inside, jnp.exp(-offset * offset / 200.0), jnp.float32(0.0))
    return weights / jnp.sum(weights, axis=1, keepdims=True)


def ring_pairs(n_shots, step):
    hi = n_shots // RING
    return [(h * RING + r, h * RING + (r + step) % RING) for h in range(hi) for r in range(RING)]


def hi_pairs(n_shots):
    hi = n_shots // RING
    return [(h * RING + r, ((h + 1) % hi) * RING + r) for h in range(hi) for r in range(RING)]


def rows(field, start, size):
    return lax.dynamic_slice_in_dim(field, start, size, axis=1)


def reduce_scatter_shots(fields, n_shots, parts=2):
    idx = lax.axis_index("shots")
    r, h = idx % RING, idx // RING
    chunk = fields[0].shape[1] // RING
    half = chunk // 2
    sub = half // parts
    fwd, bwd = ring_pairs(n_shots, 1), ring_pairs(n_shots, -1)

    def ring(fields, off):
        def take(start):
            return jnp.stack([rows(f, start + off, sub) for f in fields])

        acc_f = take(((r - 1) % RING) * chunk + h * half)
        acc_b = take(((r + 1) % RING) * chunk + (1 - h) * half)
        for t in range(1, RING):
            recv_f = lax.ppermute(acc_f, "shots", fwd)
            recv_b = lax.ppermute(acc_b, "shots", bwd)
            acc_f = recv_f + take(((r - 1 - t) % RING) * chunk + h * half)
            acc_b = recv_b + take(((r + 1 + t) % RING) * chunk + (1 - h) * half)
        return acc_f, acc_b

    out = []
    fields = tuple(fields)
    for p in range(parts):
        acc_f, acc_b = ring(fields, p * sub)
        if p + 1 < parts:
            fields, acc_f, acc_b = lax.optimization_barrier((fields, acc_f, acc_b))
        out.append(acc_f + lax.ppermute(acc_b, "shots", hi_pairs(n_shots)))
    return jnp.concatenate(out, axis=2)


def all_gather_smooth_shots(blocks, n_shots, total, parts=2):
    idx = lax.axis_index("shots")
    r, h = idx % RING, idx // RING
    chunk = total // RING
    half = chunk // 2
    sub = half // parts
    fwd, bwd = ring_pairs(n_shots, 1), ring_pairs(n_shots, -1)
    pieces, starts = [], []
    rest = blocks
    for p in range(parts):
        cur_f = rest[:, :, p * sub:(p + 1) * sub]
        cur_b = lax.ppermute(cur_f, "shots", hi_pairs(n_shots))
        if p + 1 < parts:
            rest, cur_b = lax.optimization_barrier((rest, cur_b))
        off = p * sub
        pieces += [cur_f, cur_b]
        starts += [r * chunk + h * half + off, r * chunk + (1 - h) * half + off]
        for t in range(1, RING):
            cur_f = lax.ppermute(cur_f, "shots", fwd)
            cur_b = lax.ppermute(cur_b, "shots", bwd)
            pieces += [cur_f, cur_b]
            starts += [
                ((r - t) % RING) * chunk + h * half + off,
                ((r + t) % RING) * chunk + (1 - h) * half + off,
            ]
    matrix = smoothing_matrix(total)
    matrix = jnp.concatenate(
        [lax.dynamic_slice_in_dim(matrix, s, sub, axis=1) for s in starts], axis=1
    )
    outs = []
    for k in range(blocks.shape[0]):
        joined = jnp.concatenate([p[k] for p in pieces], axis=1)
        wide = jnp.broadcast_to(matrix, (joined.shape[0],) + matrix.shape)
        outs.append(jnp.einsum("xij,xjz->xiz", wide, joined, precision=HP))
    return outs


def smooth_depth(field):
    matrix = smoothing_matrix(field.shape[-1])
    return jnp.einsum("...j,ij->...i", field, matrix, precision=HP)


def smooth_along_x(both):
    cols = lax.all_to_all(both, "slab", split_axis=2, concat_axis=1, tiled=True)
    matrix = smoothing_matrix(cols.shape[1])
    cols = jnp.einsum("ij,fjyz->fiyz", matrix, cols, precision=HP)
    return lax.all_to_all(cols, "slab", split_axis=1, concat_axis=2, tiled=True)


def make_body(n_shots):
    def body(vel_parts, den_parts, illum_parts, layer_index, depth_scale):
        total = vel_parts.shape[2]
        illum, vel, den = reduce_scatter_shots(
            [illum_parts[0], vel_parts[0], den_parts[0]], n_shots
        )
        both = jnp.stack([vel / illum, den / illum])
        both = smooth_along_x(smooth_depth(both))
        vel, den = all_gather_smooth_shots(both, n_shots, total)
        onehot = (
            layer_index[:, None] == jnp.arange(depth_scale.shape[1], dtype=jnp.int32)[None, :]
        ).astype(jnp.float32)
        per_depth = jnp.dot(depth_scale, onehot.T, precision=HP)
        vel_update = per_depth[0][None, None, :] * vel
        den_update = per_depth[1][None, None, :] * den
        return (vel_update, den_update)

    return body


def solution(mesh):
    placed = (
        P("shots", "slab", None, None),
        P("shots", "slab", None, None),
        P("shots", "slab", None, None),
        P(),
        P(),
    )
    return jax.shard_map(
        make_body(mesh.shape["shots"]),
        mesh=mesh,
        in_specs=placed,
        out_specs=(P("slab", None, None), P("slab", None, None)),
        check_vma=False,
    )
```

```python
import jax
import jax.numpy as jnp
from jax import lax
from jax.sharding import PartitionSpec as P

RADIUS = 20
HP = lax.Precision.HIGH
RING = 4


def smoothing_matrix(count):
    cells = jnp.arange(count, dtype=jnp.int32)
    offset = (cells[:, None] - cells[None, :]).astype(jnp.float32)
    inside = jnp.abs(offset) <= RADIUS
    weights = jnp.where(inside, jnp.exp(-offset * offset / 200.0), jnp.float32(0.0))
    return weights / jnp.sum(weights, axis=1, keepdims=True)


def ring_pairs(n_shots, step):
    hi = n_shots // RING
    return [(h * RING + r, h * RING + (r + step) % RING) for h in range(hi) for r in range(RING)]


def hi_pairs(n_shots):
    hi = n_shots // RING
    return [(h * RING + r, ((h + 1) % hi) * RING + r) for h in range(hi) for r in range(RING)]


def rows(field, start, size):
    return lax.dynamic_slice_in_dim(field, start, size, axis=1)


def reduce_scatter_shots(fields, n_shots, parts=2):
    idx = lax.axis_index("shots")
    r, h = idx % RING, idx // RING
    chunk = fields[0].shape[1] // RING
    half = chunk // 2
    sub = half // parts
    fwd, bwd = ring_pairs(n_shots, 1), ring_pairs(n_shots, -1)

    def ring(fields, off):
        def take(start):
            return jnp.stack([rows(f, start + off, sub) for f in fields])

        acc_f = take(((r - 1) % RING) * chunk + h * half)
        acc_b = take(((r + 1) % RING) * chunk + (1 - h) * half)
        for t in range(1, RING):
            recv_f = lax.ppermute(acc_f, "shots", fwd)
            recv_b = lax.ppermute(acc_b, "shots", bwd)
            acc_f = recv_f + take(((r - 1 - t) % RING) * chunk + h * half)
            acc_b = recv_b + take(((r + 1 + t) % RING) * chunk + (1 - h) * half)
        return acc_f, acc_b

    out = []
    fields = tuple(fields)
    for p in range(parts):
        acc_f, acc_b = ring(fields, p * sub)
        if p + 1 < parts:
            fields, acc_f, acc_b = lax.optimization_barrier((fields, acc_f, acc_b))
        out.append(acc_f + lax.ppermute(acc_b, "shots", hi_pairs(n_shots)))
    return jnp.concatenate(out, axis=2)


def all_gather_smooth_shots(blocks, n_shots, total, parts=2):
    idx = lax.axis_index("shots")
    r, h = idx % RING, idx // RING
    chunk = total // RING
    half = chunk // 2
    sub = half // parts
    fwd, bwd = ring_pairs(n_shots, 1), ring_pairs(n_shots, -1)
    pieces, starts = [], []
    rest = blocks
    for p in range(parts):
        cur_f = rest[:, :, p * sub:(p + 1) * sub]
        cur_b = lax.ppermute(cur_f, "shots", hi_pairs(n_shots))
        if p + 1 < parts:
            rest, cur_b = lax.optimization_barrier((rest, cur_b))
        off = p * sub
        pieces += [cur_f, cur_b]
        starts += [r * chunk + h * half + off, r * chunk + (1 - h) * half + off]
        for t in range(1, RING):
            cur_f = lax.ppermute(cur_f, "shots", fwd)
            cur_b = lax.ppermute(cur_b, "shots", bwd)
            pieces += [cur_f, cur_b]
            starts += [
                ((r - t) % RING) * chunk + h * half + off,
                ((r + t) % RING) * chunk + (1 - h) * half + off,
            ]
    matrix = smoothing_matrix(total)
    matrix = jnp.concatenate(
        [lax.dynamic_slice_in_dim(matrix, s, sub, axis=1) for s in starts], axis=1
    )
    outs = []
    for k in range(blocks.shape[0]):
        joined = jnp.concatenate([p[k] for p in pieces], axis=1)
        wide = jnp.broadcast_to(matrix, (joined.shape[0],) + matrix.shape)
        outs.append(jnp.einsum("xij,xjz->xiz", wide, joined, precision=HP))
    return outs


def smooth_depth(field):
    matrix = smoothing_matrix(field.shape[-1])
    return jnp.einsum("...j,ij->...i", field, matrix, precision=HP)


def smooth_along_x(both):
    cols = lax.all_to_all(both, "slab", split_axis=2, concat_axis=1, tiled=True)
    matrix = smoothing_matrix(cols.shape[1])
    cols = jnp.einsum("ij,fjyz->fiyz", matrix, cols, precision=HP)
    return lax.all_to_all(cols, "slab", split_axis=1, concat_axis=2, tiled=True)


def make_body(n_shots):
    def body(vel_parts, den_parts, illum_parts, layer_index, depth_scale):
        total = vel_parts.shape[2]
        illum, vel, den = reduce_scatter_shots(
            [illum_parts[0], vel_parts[0], den_parts[0]], n_shots
        )
        both = jnp.stack([vel / illum, den / illum])
        both = smooth_along_x(smooth_depth(both))
        vel, den = all_gather_smooth_shots(both, n_shots, total)
        onehot = (
            layer_index[:, None] == jnp.arange(depth_scale.shape[1], dtype=jnp.int32)[None, :]
        ).astype(jnp.float32)
        per_depth = jnp.dot(depth_scale, onehot.T, precision=lax.Precision.HIGHEST)
        vel_update = per_depth[0][None, None, :] * vel
        den_update = per_depth[1][None, None, :] * den
        return (vel_update, den_update)

    return body


def solution(mesh):
    placed = (
        P("shots", "slab", None, None),
        P("shots", "slab", None, None),
        P("shots", "slab", None, None),
        P(),
        P(),
    )
    return jax.shard_map(
        make_body(mesh.shape["shots"]),
        mesh=mesh,
        in_specs=placed,
        out_specs=(P("slab", None, None), P("slab", None, None)),
        check_vma=False,
    )
```

```python
import jax
import jax.numpy as jnp
from jax import lax
from jax.sharding import PartitionSpec as P

RADIUS = 20
HP = lax.Precision.HIGHEST
RING = 4


def smoothing_matrix(count):
    cells = jnp.arange(count, dtype=jnp.int32)
    offset = (cells[:, None] - cells[None, :]).astype(jnp.float32)
    inside = jnp.abs(offset) <= RADIUS
    weights = jnp.where(inside, jnp.exp(-offset * offset / 200.0), jnp.float32(0.0))
    return weights / jnp.sum(weights, axis=1, keepdims=True)


def ring_pairs(n_shots, step):
    hi = n_shots // RING
    return [(h * RING + r, h * RING + (r + step) % RING) for h in range(hi) for r in range(RING)]


def hi_pairs(n_shots):
    hi = n_shots // RING
    return [(h * RING + r, ((h + 1) % hi) * RING + r) for h in range(hi) for r in range(RING)]


def rows(field, start, size):
    return lax.dynamic_slice_in_dim(field, start, size, axis=1)


def reduce_scatter_shots(fields, n_shots, parts=2):
    idx = lax.axis_index("shots")
    r, h = idx % RING, idx // RING
    chunk = fields[0].shape[1] // RING
    half = chunk // 2
    sub = half // parts
    fwd, bwd = ring_pairs(n_shots, 1), ring_pairs(n_shots, -1)

    def ring(fields, off, gate):
        def take(start):
            return jnp.stack([rows(f, start + off, sub) for f in fields])

        acc_f = take(((r - 1) % RING) * chunk + h * half)
        acc_b = take(((r + 1) % RING) * chunk + (1 - h) * half)
        for t in range(1, RING):
            recv_f = lax.ppermute(acc_f, "shots", fwd)
            recv_b = lax.ppermute(acc_b, "shots", bwd)
            if t == 2 and gate is not None:
                recv_f, recv_b, gate = lax.optimization_barrier((recv_f, recv_b, gate))
            acc_f = recv_f + take(((r - 1 - t) % RING) * chunk + h * half)
            acc_b = recv_b + take(((r + 1 + t) % RING) * chunk + (1 - h) * half)
        return acc_f, acc_b

    out = []
    fields = tuple(fields)
    gate = None
    for p in range(parts):
        acc_f, acc_b = ring(fields, p * sub, gate)
        if p + 1 < parts:
            fields, acc_f, acc_b = lax.optimization_barrier((fields, acc_f, acc_b))
        gate = lax.ppermute(acc_b, "shots", hi_pairs(n_shots))
        out.append(acc_f + gate)
    return jnp.concatenate(out, axis=2)


def all_gather_smooth_shots(blocks, n_shots, total, parts=2):
    idx = lax.axis_index("shots")
    r, h = idx % RING, idx // RING
    chunk = total // RING
    half = chunk // 2
    sub = half // parts
    fwd, bwd = ring_pairs(n_shots, 1), ring_pairs(n_shots, -1)
    pieces, starts = [], []
    rest = blocks
    for p in range(parts):
        cur_f = rest[:, :, p * sub:(p + 1) * sub]
        cur_b = lax.ppermute(cur_f, "shots", hi_pairs(n_shots))
        if p + 1 < parts:
            rest, cur_b = lax.optimization_barrier((rest, cur_b))
        off = p * sub
        pieces += [cur_f, cur_b]
        starts += [r * chunk + h * half + off, r * chunk + (1 - h) * half + off]
        for t in range(1, RING):
            cur_f = lax.ppermute(cur_f, "shots", fwd)
            cur_b = lax.ppermute(cur_b, "shots", bwd)
            pieces += [cur_f, cur_b]
            starts += [
                ((r - t) % RING) * chunk + h * half + off,
                ((r + t) % RING) * chunk + (1 - h) * half + off,
            ]
    matrix = smoothing_matrix(total)
    matrix = jnp.concatenate(
        [lax.dynamic_slice_in_dim(matrix, s, sub, axis=1) for s in starts], axis=1
    )
    outs = []
    for k in range(blocks.shape[0]):
        joined = jnp.concatenate([p[k] for p in pieces], axis=1)
        wide = jnp.broadcast_to(matrix, (joined.shape[0],) + matrix.shape)
        outs.append(jnp.einsum("xij,xjz->xiz", wide, joined, precision=HP))
    return outs


def smooth_depth(field):
    matrix = smoothing_matrix(field.shape[-1])
    return jnp.einsum("...j,ij->...i", field, matrix, precision=HP)


def smooth_along_x(both):
    cols = lax.all_to_all(both, "slab", split_axis=2, concat_axis=1, tiled=True)
    matrix = smoothing_matrix(cols.shape[1])
    cols = jnp.einsum("ij,fjyz->fiyz", matrix, cols, precision=HP)
    return lax.all_to_all(cols, "slab", split_axis=1, concat_axis=2, tiled=True)


def make_body(n_shots):
    def body(vel_parts, den_parts, illum_parts, layer_index, depth_scale):
        total = vel_parts.shape[2]
        illum, vel, den = reduce_scatter_shots(
            [illum_parts[0], vel_parts[0], den_parts[0]], n_shots
        )
        both = jnp.stack([vel / illum, den / illum])
        both = smooth_along_x(smooth_depth(both))
        vel, den = all_gather_smooth_shots(both, n_shots, total)
        onehot = (
            layer_index[:, None] == jnp.arange(depth_scale.shape[1], dtype=jnp.int32)[None, :]
        ).astype(jnp.float32)
        per_depth = jnp.dot(depth_scale, onehot.T, precision=HP)
        vel_update = per_depth[0][None, None, :] * vel
        den_update = per_depth[1][None, None, :] * den
        return (vel_update, den_update)

    return body


def solution(mesh):
    placed = (
        P("shots", "slab", None, None),
        P("shots", "slab", None, None),
        P("shots", "slab", None, None),
        P(),
        P(),
    )
    return jax.shard_map(
        make_body(mesh.shape["shots"]),
        mesh=mesh,
        in_specs=placed,
        out_specs=(P("slab", None, None), P("slab", None, None)),
        check_vma=False,
    )
```

```python
import jax
import jax.numpy as jnp
from jax import lax
from jax.sharding import PartitionSpec as P

RADIUS = 20
HP = lax.Precision.HIGHEST
RING = 4


def smoothing_matrix(count):
    cells = jnp.arange(count, dtype=jnp.int32)
    offset = (cells[:, None] - cells[None, :]).astype(jnp.float32)
    inside = jnp.abs(offset) <= RADIUS
    weights = jnp.where(inside, jnp.exp(-offset * offset / 200.0), jnp.float32(0.0))
    return weights / jnp.sum(weights, axis=1, keepdims=True)


def ring_pairs(n_shots, step):
    hi = n_shots // RING
    return [(h * RING + r, h * RING + (r + step) % RING) for h in range(hi) for r in range(RING)]


def hi_pairs(n_shots):
    hi = n_shots // RING
    return [(h * RING + r, ((h + 1) % hi) * RING + r) for h in range(hi) for r in range(RING)]


def rows(field, start, size):
    return lax.dynamic_slice_in_dim(field, start, size, axis=1)


def reduce_scatter_shots(fields, n_shots, parts=2):
    idx = lax.axis_index("shots")
    r, h = idx % RING, idx // RING
    chunk = fields[0].shape[1] // RING
    half = chunk // 2
    sub = half // parts
    fwd, bwd = ring_pairs(n_shots, 1), ring_pairs(n_shots, -1)

    def ring(fields, off, gate):
        def take(start):
            return jnp.stack([rows(f, start + off, sub) for f in fields])

        acc_f = take(((r - 1) % RING) * chunk + h * half)
        acc_b = take(((r + 1) % RING) * chunk + (1 - h) * half)
        for t in range(1, RING):
            recv_f = lax.ppermute(acc_f, "shots", fwd)
            recv_b = lax.ppermute(acc_b, "shots", bwd)
            if t == 2 and gate is not None:
                recv_f, recv_b, gate = lax.optimization_barrier((recv_f, recv_b, gate))
            acc_f = recv_f + take(((r - 1 - t) % RING) * chunk + h * half)
            acc_b = recv_b + take(((r + 1 + t) % RING) * chunk + (1 - h) * half)
        return acc_f, acc_b

    out = []
    fields = tuple(fields)
    gate = None
    for p in range(parts):
        acc_f, acc_b = ring(fields, p * sub, gate)
        if p + 1 < parts:
            fields, acc_f, acc_b = lax.optimization_barrier((fields, acc_f, acc_b))
        gate = lax.ppermute(acc_b, "shots", hi_pairs(n_shots))
        out.append(acc_f + gate)
    return out


def all_gather_smooth_shots(blocks, n_shots, total):
    idx = lax.axis_index("shots")
    r, h = idx % RING, idx // RING
    chunk = total // RING
    half = chunk // 2
    parts = len(blocks)
    sub = half // parts
    fwd, bwd = ring_pairs(n_shots, 1), ring_pairs(n_shots, -1)
    pieces, starts = [], []
    rest = tuple(blocks)
    for p in range(parts):
        cur_f = rest[p]
        cur_b = lax.ppermute(cur_f, "shots", hi_pairs(n_shots))
        if p + 1 < parts:
            rest, cur_b = lax.optimization_barrier((rest, cur_b))
        off = p * sub
        pieces += [cur_f, cur_b]
        starts += [r * chunk + h * half + off, r * chunk + (1 - h) * half + off]
        for t in range(1, RING):
            cur_f = lax.ppermute(cur_f, "shots", fwd)
            cur_b = lax.ppermute(cur_b, "shots", bwd)
            pieces += [cur_f, cur_b]
            starts += [
                ((r - t) % RING) * chunk + h * half + off,
                ((r + t) % RING) * chunk + (1 - h) * half + off,
            ]
    matrix = smoothing_matrix(total)
    matrix = jnp.concatenate(
        [lax.dynamic_slice_in_dim(matrix, s, sub, axis=1) for s in starts], axis=1
    )
    outs = []
    for k in range(blocks[0].shape[0]):
        joined = jnp.concatenate([p[k] for p in pieces], axis=1)
        wide = jnp.broadcast_to(matrix, (joined.shape[0],) + matrix.shape)
        outs.append(jnp.einsum("xij,xjz->xiz", wide, joined, precision=HP))
    return outs


def smooth_depth(field):
    matrix = smoothing_matrix(field.shape[-1])
    return jnp.einsum("...j,ij->...i", field, matrix, precision=HP)


def smooth_along_x(both):
    cols = lax.all_to_all(both, "slab", split_axis=2, concat_axis=1, tiled=True)
    matrix = smoothing_matrix(cols.shape[1])
    cols = jnp.einsum("ij,fjyz->fiyz", matrix, cols, precision=HP)
    return lax.all_to_all(cols, "slab", split_axis=1, concat_axis=2, tiled=True)


def make_body(n_shots):
    def body(vel_parts, den_parts, illum_parts, layer_index, depth_scale):
        total = vel_parts.shape[2]
        parts = []
        for illum, vel, den in reduce_scatter_shots(
            [illum_parts[0], vel_parts[0], den_parts[0]], n_shots
        ):
            both = jnp.stack([vel / illum, den / illum])
            parts.append(smooth_along_x(smooth_depth(both)))
        vel, den = all_gather_smooth_shots(parts, n_shots, total)
        onehot = (
            layer_index[:, None] == jnp.arange(depth_scale.shape[1], dtype=jnp.int32)[None, :]
        ).astype(jnp.float32)
        per_depth = jnp.dot(depth_scale, onehot.T, precision=HP)
        vel_update = per_depth[0][None, None, :] * vel
        den_update = per_depth[1][None, None, :] * den
        return (vel_update, den_update)

    return body


def solution(mesh):
    placed = (
        P("shots", "slab", None, None),
        P("shots", "slab", None, None),
        P("shots", "slab", None, None),
        P(),
        P(),
    )
    return jax.shard_map(
        make_body(mesh.shape["shots"]),
        mesh=mesh,
        in_specs=placed,
        out_specs=(P("slab", None, None), P("slab", None, None)),
        check_vma=False,
    )
```

```python
import jax
import jax.numpy as jnp
from jax import lax
from jax.sharding import PartitionSpec as P

RADIUS = 20
HP = lax.Precision.HIGHEST
RING = 4


def smoothing_matrix(count):
    cells = jnp.arange(count, dtype=jnp.int32)
    offset = (cells[:, None] - cells[None, :]).astype(jnp.float32)
    inside = jnp.abs(offset) <= RADIUS
    weights = jnp.where(inside, jnp.exp(-offset * offset / 200.0), jnp.float32(0.0))
    return weights / jnp.sum(weights, axis=1, keepdims=True)


def ring_pairs(n_shots, step):
    hi = n_shots // RING
    return [(h * RING + r, h * RING + (r + step) % RING) for h in range(hi) for r in range(RING)]


def hi_pairs(n_shots):
    hi = n_shots // RING
    return [(h * RING + r, ((h + 1) % hi) * RING + r) for h in range(hi) for r in range(RING)]


def rows(field, start, size):
    return lax.dynamic_slice_in_dim(field, start, size, axis=1)


def reduce_scatter_shots(fields, n_shots, parts=2):
    idx = lax.axis_index("shots")
    r, h = idx % RING, idx // RING
    chunk = fields[0].shape[1] // RING
    half = chunk // 2
    sub = half // parts
    fwd, bwd = ring_pairs(n_shots, 1), ring_pairs(n_shots, -1)

    def ring(fields, off, gate):
        def take(start):
            return jnp.stack([rows(f, start + off, sub) for f in fields])

        acc_f = take(((r - 1) % RING) * chunk + h * half)
        acc_b = take(((r + 1) % RING) * chunk + (1 - h) * half)
        for t in range(1, RING):
            recv_f = lax.ppermute(acc_f, "shots", fwd)
            recv_b = lax.ppermute(acc_b, "shots", bwd)
            if t == 2 and gate is not None:
                recv_f, recv_b, gate = lax.optimization_barrier((recv_f, recv_b, gate))
            acc_f = recv_f + take(((r - 1 - t) % RING) * chunk + h * half)
            acc_b = recv_b + take(((r + 1 + t) % RING) * chunk + (1 - h) * half)
        return acc_f, acc_b

    out = []
    fields = tuple(fields)
    gate = None
    for p in range(parts):
        acc_f, acc_b = ring(fields, p * sub, gate)
        if p + 1 < parts:
            fields, acc_f, acc_b = lax.optimization_barrier((fields, acc_f, acc_b))
        gate = lax.ppermute(acc_b, "shots", hi_pairs(n_shots))
        out.append(acc_f + gate)
    return jnp.concatenate(out, axis=2)


def all_gather_smooth_shots(blocks, n_shots, total, parts=2):
    idx = lax.axis_index("shots")
    r, h = idx % RING, idx // RING
    chunk = total // RING
    half = chunk // 2
    sub = half // parts
    fwd, bwd = ring_pairs(n_shots, 1), ring_pairs(n_shots, -1)
    pieces, starts = [], []
    rest = blocks
    for p in range(parts):
        cur_f = rest[:, :, p * sub:(p + 1) * sub]
        cur_b = lax.ppermute(cur_f, "shots", hi_pairs(n_shots))
        if p + 1 < parts:
            rest, cur_b = lax.optimization_barrier((rest, cur_b))
        off = p * sub
        pieces += [cur_f, cur_b]
        starts += [r * chunk + h * half + off, r * chunk + (1 - h) * half + off]
        for t in range(1, RING):
            cur_f = lax.ppermute(cur_f, "shots", fwd)
            cur_b = lax.ppermute(cur_b, "shots", bwd)
            pieces += [cur_f, cur_b]
            starts += [
                ((r - t) % RING) * chunk + h * half + off,
                ((r + t) % RING) * chunk + (1 - h) * half + off,
            ]
    matrix = smoothing_matrix(total)
    matrix = jnp.concatenate(
        [lax.dynamic_slice_in_dim(matrix, s, sub, axis=1) for s in starts], axis=1
    )
    outs = []
    for k in range(blocks.shape[0]):
        joined = jnp.concatenate([p[k] for p in pieces], axis=1)
        wide = jnp.broadcast_to(matrix, (joined.shape[0],) + matrix.shape)
        outs.append(jnp.einsum("xij,xjz->xiz", wide, joined, precision=HP))
    return outs


def smooth_depth(field):
    matrix = smoothing_matrix(field.shape[-1])
    return jnp.einsum("...j,ij->...i", field, matrix, precision=HP)


def smooth_along_x(both):
    cols = lax.all_to_all(both, "slab", split_axis=2, concat_axis=1, tiled=True)
    matrix = smoothing_matrix(cols.shape[1])
    cols = jnp.einsum("ij,fjyz->fiyz", matrix, cols, precision=HP)
    return lax.all_to_all(cols, "slab", split_axis=1, concat_axis=2, tiled=True)


def make_body(n_shots):
    def body(vel_parts, den_parts, illum_parts, layer_index, depth_scale):
        total = vel_parts.shape[2]
        illum, vel, den = reduce_scatter_shots(
            [illum_parts[0], vel_parts[0], den_parts[0]], n_shots
        )
        both = jnp.stack([vel / illum, den / illum])
        both = smooth_along_x(smooth_depth(both))
        vel, den = all_gather_smooth_shots(both, n_shots, total, parts=1)
        onehot = (
            layer_index[:, None] == jnp.arange(depth_scale.shape[1], dtype=jnp.int32)[None, :]
        ).astype(jnp.float32)
        per_depth = jnp.dot(depth_scale, onehot.T, precision=HP)
        vel_update = per_depth[0][None, None, :] * vel
        den_update = per_depth[1][None, None, :] * den
        return (vel_update, den_update)

    return body


def solution(mesh):
    placed = (
        P("shots", "slab", None, None),
        P("shots", "slab", None, None),
        P("shots", "slab", None, None),
        P(),
        P(),
    )
    return jax.shard_map(
        make_body(mesh.shape["shots"]),
        mesh=mesh,
        in_specs=placed,
        out_specs=(P("slab", None, None), P("slab", None, None)),
        check_vma=False,
    )
```

```python
import jax
import jax.numpy as jnp
from jax import lax
from jax.sharding import PartitionSpec as P

RADIUS = 20
HP = lax.Precision.HIGHEST
RING = 4


def smoothing_matrix(count):
    cells = jnp.arange(count, dtype=jnp.int32)
    offset = (cells[:, None] - cells[None, :]).astype(jnp.float32)
    inside = jnp.abs(offset) <= RADIUS
    weights = jnp.where(inside, jnp.exp(-offset * offset / 200.0), jnp.float32(0.0))
    return weights / jnp.sum(weights, axis=1, keepdims=True)


def ring_pairs(n_shots, step):
    hi = n_shots // RING
    return [(h * RING + r, h * RING + (r + step) % RING) for h in range(hi) for r in range(RING)]


def hi_pairs(n_shots):
    hi = n_shots // RING
    return [(h * RING + r, ((h + 1) % hi) * RING + r) for h in range(hi) for r in range(RING)]


def rows(field, start, size):
    return lax.dynamic_slice_in_dim(field, start, size, axis=1)


def ring_sum(fields, starts, size, n_shots):
    idx = lax.axis_index("shots")
    r = idx % RING
    q = size // 2
    fwd, bwd = ring_pairs(n_shots, 1), ring_pairs(n_shots, -1)

    def take(start):
        return jnp.stack([rows(f, start, q) for f in fields])

    acc_f = take(starts((r - 1) % RING))
    acc_b = take(starts((r + 1) % RING) + q)
    for t in range(1, RING):
        recv_f = lax.ppermute(acc_f, "shots", fwd)
        recv_b = lax.ppermute(acc_b, "shots", bwd)
        acc_f = recv_f + take(starts((r - 1 - t) % RING))
        acc_b = recv_b + take(starts((r + 1 + t) % RING) + q)
    return jnp.concatenate([acc_f, acc_b], axis=2)


def reduce_scatter_shots(fields, n_shots):
    idx = lax.axis_index("shots")
    h = idx // RING
    chunk = fields[0].shape[1] // RING
    half = chunk // 2
    theirs = ring_sum(fields, lambda c: c * chunk + (1 - h) * half, half, n_shots)
    fields, theirs = lax.optimization_barrier((tuple(fields), theirs))
    got = lax.ppermute(theirs, "shots", hi_pairs(n_shots))
    mine = ring_sum(fields, lambda c: c * chunk + h * half, half, n_shots)
    return mine + got


def all_gather_smooth_shots(blocks, n_shots, total):
    idx = lax.axis_index("shots")
    r, h = idx % RING, idx // RING
    chunk = total // RING
    half = chunk // 2
    q = half // 2
    fwd, bwd = ring_pairs(n_shots, 1), ring_pairs(n_shots, -1)
    other = lax.ppermute(blocks, "shots", hi_pairs(n_shots))
    pieces, starts = [], []
    for block, side in ((blocks, h), (other, 1 - h)):
        cur_f, cur_b = block[:, :, :q], block[:, :, q:]
        pieces += [cur_f, cur_b]
        starts += [r * chunk + side * half, r * chunk + side * half + q]
        for t in range(1, RING):
            cur_f = lax.ppermute(cur_f, "shots", fwd)
            cur_b = lax.ppermute(cur_b, "shots", bwd)
            pieces += [cur_f, cur_b]
            starts += [((r - t) % RING) * chunk + side * half, ((r + t) % RING) * chunk + side * half + q]
    matrix = smoothing_matrix(total)
    matrix = jnp.concatenate(
        [lax.dynamic_slice_in_dim(matrix, s, q, axis=1) for s in starts], axis=1
    )
    outs = []
    for k in range(blocks.shape[0]):
        joined = jnp.concatenate([p[k] for p in pieces], axis=1)
        wide = jnp.broadcast_to(matrix, (joined.shape[0],) + matrix.shape)
        outs.append(jnp.einsum("xij,xjz->xiz", wide, joined, precision=HP))
    return outs


def smooth_depth(field):
    matrix = smoothing_matrix(field.shape[-1])
    return jnp.einsum("...j,ij->...i", field, matrix, precision=HP)


def smooth_along_x(both):
    cols = lax.all_to_all(both, "slab", split_axis=2, concat_axis=1, tiled=True)
    matrix = smoothing_matrix(cols.shape[1])
    cols = jnp.einsum("ij,fjyz->fiyz", matrix, cols, precision=HP)
    return lax.all_to_all(cols, "slab", split_axis=1, concat_axis=2, tiled=True)


def make_body(n_shots):
    def body(vel_parts, den_parts, illum_parts, layer_index, depth_scale):
        total = vel_parts.shape[2]
        illum, vel, den = reduce_scatter_shots(
            [illum_parts[0], vel_parts[0], den_parts[0]], n_shots
        )
        both = jnp.stack([vel / illum, den / illum])
        both = smooth_along_x(smooth_depth(both))
        vel, den = all_gather_smooth_shots(both, n_shots, total)
        onehot = (
            layer_index[:, None] == jnp.arange(depth_scale.shape[1], dtype=jnp.int32)[None, :]
        ).astype(jnp.float32)
        per_depth = jnp.dot(depth_scale, onehot.T, precision=HP)
        vel_update = per_depth[0][None, None, :] * vel
        den_update = per_depth[1][None, None, :] * den
        return (vel_update, den_update)

    return body


def solution(mesh):
    placed = (
        P("shots", "slab", None, None),
        P("shots", "slab", None, None),
        P("shots", "slab", None, None),
        P(),
        P(),
    )
    return jax.shard_map(
        make_body(mesh.shape["shots"]),
        mesh=mesh,
        in_specs=placed,
        out_specs=(P("slab", None, None), P("slab", None, None)),
        check_vma=False,
    )
```

```python
import jax
import jax.numpy as jnp
from jax import lax
from jax.sharding import PartitionSpec as P

RADIUS = 20
HP = lax.Precision.HIGHEST
RING = 4


def smoothing_matrix(count):
    cells = jnp.arange(count, dtype=jnp.int32)
    offset = (cells[:, None] - cells[None, :]).astype(jnp.float32)
    inside = jnp.abs(offset) <= RADIUS
    weights = jnp.where(inside, jnp.exp(-offset * offset / 200.0), jnp.float32(0.0))
    return weights / jnp.sum(weights, axis=1, keepdims=True)


def ring_pairs(n_shots, step):
    hi = n_shots // RING
    return [(h * RING + r, h * RING + (r + step) % RING) for h in range(hi) for r in range(RING)]


def hi_pairs(n_shots):
    hi = n_shots // RING
    return [(h * RING + r, ((h + 1) % hi) * RING + r) for h in range(hi) for r in range(RING)]


def rows(field, start, size):
    return lax.dynamic_slice_in_dim(field, start, size, axis=1)


def ring_sum(fields, starts, size, n_shots, gate=None):
    idx = lax.axis_index("shots")
    r = idx % RING
    q = size // 2
    fwd, bwd = ring_pairs(n_shots, 1), ring_pairs(n_shots, -1)

    def take(start):
        return jnp.stack([rows(f, start, q) for f in fields])

    acc_f = take(starts((r - 1) % RING))
    acc_b = take(starts((r + 1) % RING) + q)
    for t in range(1, RING):
        recv_f = lax.ppermute(acc_f, "shots", fwd)
        recv_b = lax.ppermute(acc_b, "shots", bwd)
        if gate is not None and t == RING - 1:
            recv_f, recv_b, gate = lax.optimization_barrier((recv_f, recv_b, gate))
        acc_f = recv_f + take(starts((r - 1 - t) % RING))
        acc_b = recv_b + take(starts((r + 1 + t) % RING) + q)
    return jnp.concatenate([acc_f, acc_b], axis=2)


def reduce_scatter_shots(fields, n_shots):
    idx = lax.axis_index("shots")
    h = idx // RING
    chunk = fields[0].shape[1] // RING
    half = chunk // 2
    theirs = ring_sum(fields, lambda c: c * chunk + (1 - h) * half, half, n_shots)
    fields, theirs = lax.optimization_barrier((tuple(fields), theirs))
    got = lax.ppermute(theirs, "shots", hi_pairs(n_shots))
    mine = ring_sum(fields, lambda c: c * chunk + h * half, half, n_shots, gate=got)
    return mine + got


def all_gather_smooth_shots(blocks, n_shots, total):
    idx = lax.axis_index("shots")
    r, h = idx % RING, idx // RING
    chunk = total // RING
    half = chunk // 2
    q = half // 2
    fwd, bwd = ring_pairs(n_shots, 1), ring_pairs(n_shots, -1)
    other = lax.ppermute(blocks, "shots", hi_pairs(n_shots))
    pieces, starts = [], []
    for block, side in ((blocks, h), (other, 1 - h)):
        cur_f, cur_b = block[:, :, :q], block[:, :, q:]
        pieces += [cur_f, cur_b]
        starts += [r * chunk + side * half, r * chunk + side * half + q]
        for t in range(1, RING):
            cur_f = lax.ppermute(cur_f, "shots", fwd)
            cur_b = lax.ppermute(cur_b, "shots", bwd)
            pieces += [cur_f, cur_b]
            starts += [((r - t) % RING) * chunk + side * half, ((r + t) % RING) * chunk + side * half + q]
    matrix = smoothing_matrix(total)
    matrix = jnp.concatenate(
        [lax.dynamic_slice_in_dim(matrix, s, q, axis=1) for s in starts], axis=1
    )
    outs = []
    for k in range(blocks.shape[0]):
        joined = jnp.concatenate([p[k] for p in pieces], axis=1)
        wide = jnp.broadcast_to(matrix, (joined.shape[0],) + matrix.shape)
        outs.append(jnp.einsum("xij,xjz->xiz", wide, joined, precision=HP))
    return outs


def smooth_depth(field):
    matrix = smoothing_matrix(field.shape[-1])
    return jnp.einsum("...j,ij->...i", field, matrix, precision=HP)


def smooth_along_x(both):
    cols = lax.all_to_all(both, "slab", split_axis=2, concat_axis=1, tiled=True)
    matrix = smoothing_matrix(cols.shape[1])
    cols = jnp.einsum("ij,fjyz->fiyz", matrix, cols, precision=HP)
    return lax.all_to_all(cols, "slab", split_axis=1, concat_axis=2, tiled=True)


def make_body(n_shots):
    def body(vel_parts, den_parts, illum_parts, layer_index, depth_scale):
        total = vel_parts.shape[2]
        illum, vel, den = reduce_scatter_shots(
            [illum_parts[0], vel_parts[0], den_parts[0]], n_shots
        )
        both = jnp.stack([vel / illum, den / illum])
        both = smooth_along_x(smooth_depth(both))
        vel, den = all_gather_smooth_shots(both, n_shots, total)
        onehot = (
            layer_index[:, None] == jnp.arange(depth_scale.shape[1], dtype=jnp.int32)[None, :]
        ).astype(jnp.float32)
        per_depth = jnp.dot(depth_scale, onehot.T, precision=HP)
        vel_update = per_depth[0][None, None, :] * vel
        den_update = per_depth[1][None, None, :] * den
        return (vel_update, den_update)

    return body


def solution(mesh):
    placed = (
        P("shots", "slab", None, None),
        P("shots", "slab", None, None),
        P("shots", "slab", None, None),
        P(),
        P(),
    )
    return jax.shard_map(
        make_body(mesh.shape["shots"]),
        mesh=mesh,
        in_specs=placed,
        out_specs=(P("slab", None, None), P("slab", None, None)),
        check_vma=False,
    )
```

```python
import jax
import jax.numpy as jnp
from jax import lax
from jax.sharding import PartitionSpec as P

RADIUS = 20
HP = lax.Precision.HIGHEST
RING = 4


def smoothing_matrix(count):
    cells = jnp.arange(count, dtype=jnp.int32)
    offset = (cells[:, None] - cells[None, :]).astype(jnp.float32)
    inside = jnp.abs(offset) <= RADIUS
    weights = jnp.where(inside, jnp.exp(-offset * offset / 200.0), jnp.float32(0.0))
    return weights / jnp.sum(weights, axis=1, keepdims=True)


def ring_pairs(n_shots, step):
    hi = n_shots // RING
    return [(h * RING + r, h * RING + (r + step) % RING) for h in range(hi) for r in range(RING)]


def hi_pairs(n_shots):
    hi = n_shots // RING
    return [(h * RING + r, ((h + 1) % hi) * RING + r) for h in range(hi) for r in range(RING)]


def rows(field, start, size):
    return lax.dynamic_slice_in_dim(field, start, size, axis=1)


def ring_sum(fields, starts, size, n_shots):
    idx = lax.axis_index("shots")
    r = idx % RING
    q = size // 2
    fwd, bwd = ring_pairs(n_shots, 1), ring_pairs(n_shots, -1)

    def take(start):
        return jnp.stack([rows(f, start, q) for f in fields])

    acc_f = take(starts((r - 1) % RING))
    acc_b = take(starts((r + 1) % RING) + q)
    for t in range(1, RING):
        recv_f = lax.ppermute(acc_f, "shots", fwd)
        recv_b = lax.ppermute(acc_b, "shots", bwd)
        acc_f = recv_f + take(starts((r - 1 - t) % RING))
        acc_b = recv_b + take(starts((r + 1 + t) % RING) + q)
    return jnp.concatenate([acc_f, acc_b], axis=2)


def reduce_scatter_shots(fields, n_shots):
    idx = lax.axis_index("shots")
    h = idx // RING
    chunk = fields[0].shape[1] // RING
    half = chunk // 2
    theirs = ring_sum(fields, lambda c: c * chunk + (1 - h) * half, half, n_shots)
    fields, theirs = lax.optimization_barrier((tuple(fields), theirs))
    got = lax.ppermute(theirs, "shots", hi_pairs(n_shots))
    mine = ring_sum(fields, lambda c: c * chunk + h * half, half, n_shots)
    return mine + got


def all_gather_smooth_shots(blocks, n_shots, total):
    idx = lax.axis_index("shots")
    r, h = idx % RING, idx // RING
    chunk = total // RING
    half = chunk // 2
    q = half // 2
    fwd, bwd = ring_pairs(n_shots, 1), ring_pairs(n_shots, -1)
    matrix = smoothing_matrix(total)

    def contract(pieces, starts):
        cols = jnp.concatenate(
            [lax.dynamic_slice_in_dim(matrix, s, q, axis=1) for s in starts], axis=1
        )
        outs = []
        for k in range(blocks.shape[0]):
            joined = jnp.concatenate([p[k] for p in pieces], axis=1)
            wide = jnp.broadcast_to(cols, (joined.shape[0],) + cols.shape)
            outs.append(jnp.einsum("xij,xjz->xiz", wide, joined, precision=HP))
        return outs

    other = lax.ppermute(blocks, "shots", hi_pairs(n_shots))
    early = None
    for block, side in ((blocks, h), (other, 1 - h)):
        cur_f, cur_b = block[:, :, :q], block[:, :, q:]
        pieces = [cur_f, cur_b]
        starts = [r * chunk + side * half, r * chunk + side * half + q]
        for t in range(1, RING):
            cur_f = lax.ppermute(cur_f, "shots", fwd)
            cur_b = lax.ppermute(cur_b, "shots", bwd)
            if early is not None and t == RING - 1:
                cur_f, cur_b, early = lax.optimization_barrier((cur_f, cur_b, early))
            pieces += [cur_f, cur_b]
            starts += [((r - t) % RING) * chunk + side * half, ((r + t) % RING) * chunk + side * half + q]
        if early is None:
            early = contract(pieces, starts)
        else:
            late = contract(pieces, starts)
    return [a + b for a, b in zip(early, late)]


def smooth_depth(field):
    matrix = smoothing_matrix(field.shape[-1])
    return jnp.einsum("...j,ij->...i", field, matrix, precision=HP)


def smooth_along_x(both):
    cols = lax.all_to_all(both, "slab", split_axis=2, concat_axis=1, tiled=True)
    matrix = smoothing_matrix(cols.shape[1])
    cols = jnp.einsum("ij,fjyz->fiyz", matrix, cols, precision=HP)
    return lax.all_to_all(cols, "slab", split_axis=1, concat_axis=2, tiled=True)


def make_body(n_shots):
    def body(vel_parts, den_parts, illum_parts, layer_index, depth_scale):
        total = vel_parts.shape[2]
        illum, vel, den = reduce_scatter_shots(
            [illum_parts[0], vel_parts[0], den_parts[0]], n_shots
        )
        both = jnp.stack([vel / illum, den / illum])
        both = smooth_along_x(smooth_depth(both))
        vel, den = all_gather_smooth_shots(both, n_shots, total)
        onehot = (
            layer_index[:, None] == jnp.arange(depth_scale.shape[1], dtype=jnp.int32)[None, :]
        ).astype(jnp.float32)
        per_depth = jnp.dot(depth_scale, onehot.T, precision=HP)
        vel_update = per_depth[0][None, None, :] * vel
        den_update = per_depth[1][None, None, :] * den
        return (vel_update, den_update)

    return body


def solution(mesh):
    placed = (
        P("shots", "slab", None, None),
        P("shots", "slab", None, None),
        P("shots", "slab", None, None),
        P(),
        P(),
    )
    return jax.shard_map(
        make_body(mesh.shape["shots"]),
        mesh=mesh,
        in_specs=placed,
        out_specs=(P("slab", None, None), P("slab", None, None)),
        check_vma=False,
    )
```

```python
import jax
import jax.numpy as jnp
from jax import lax
from jax.sharding import PartitionSpec as P

RADIUS = 20
HP = lax.Precision.HIGHEST
RING = 4


def smoothing_matrix(count):
    cells = jnp.arange(count, dtype=jnp.int32)
    offset = (cells[:, None] - cells[None, :]).astype(jnp.float32)
    inside = jnp.abs(offset) <= RADIUS
    weights = jnp.where(inside, jnp.exp(-offset * offset / 200.0), jnp.float32(0.0))
    return weights / jnp.sum(weights, axis=1, keepdims=True)


def ring_pairs(n_shots, step):
    hi = n_shots // RING
    return [(h * RING + r, h * RING + (r + step) % RING) for h in range(hi) for r in range(RING)]


def hi_pairs(n_shots):
    hi = n_shots // RING
    return [(h * RING + r, ((h + 1) % hi) * RING + r) for h in range(hi) for r in range(RING)]


def rows(field, start, size):
    return lax.dynamic_slice_in_dim(field, start, size, axis=1)


def ring_sum(fields, starts, size, n_shots, gates=None):
    idx = lax.axis_index("shots")
    r = idx % RING
    q = size // 2
    fwd, bwd = ring_pairs(n_shots, 1), ring_pairs(n_shots, -1)

    def take(start):
        return jnp.stack([rows(f, start, q) for f in fields])

    acc_f = take(starts((r - 1) % RING))
    acc_b = take(starts((r + 1) % RING) + q)
    for t in range(1, RING):
        recv_f = lax.ppermute(acc_f, "shots", fwd)
        recv_b = lax.ppermute(acc_b, "shots", bwd)
        if gates is not None and t in gates:
            recv_f, recv_b, gates[t] = lax.optimization_barrier((recv_f, recv_b, gates[t]))
        acc_f = recv_f + take(starts((r - 1 - t) % RING))
        acc_b = recv_b + take(starts((r + 1 + t) % RING) + q)
    return jnp.concatenate([acc_f, acc_b], axis=2)


def reduce_scatter_shots(fields, n_shots):
    idx = lax.axis_index("shots")
    h = idx // RING
    chunk = fields[0].shape[1] // RING
    half = chunk // 2
    theirs = ring_sum(fields, lambda c: c * chunk + (1 - h) * half, half, n_shots)
    fields, theirs = lax.optimization_barrier((tuple(fields), theirs))
    q = half // 2
    gates = {
        RING - 2: lax.ppermute(theirs[:, :, :q], "shots", hi_pairs(n_shots)),
        RING - 1: lax.ppermute(theirs[:, :, q:], "shots", hi_pairs(n_shots)),
    }
    mine = ring_sum(fields, lambda c: c * chunk + h * half, half, n_shots, gates)
    return mine + jnp.concatenate([gates[RING - 2], gates[RING - 1]], axis=2)


def all_gather_smooth_shots(blocks, n_shots, total):
    idx = lax.axis_index("shots")
    r, h = idx % RING, idx // RING
    chunk = total // RING
    half = chunk // 2
    q = half // 2
    fwd, bwd = ring_pairs(n_shots, 1), ring_pairs(n_shots, -1)
    other = lax.ppermute(blocks, "shots", hi_pairs(n_shots))
    pieces, starts = [], []
    for block, side in ((blocks, h), (other, 1 - h)):
        cur_f, cur_b = block[:, :, :q], block[:, :, q:]
        pieces += [cur_f, cur_b]
        starts += [r * chunk + side * half, r * chunk + side * half + q]
        for t in range(1, RING):
            cur_f = lax.ppermute(cur_f, "shots", fwd)
            cur_b = lax.ppermute(cur_b, "shots", bwd)
            pieces += [cur_f, cur_b]
            starts += [((r - t) % RING) * chunk + side * half, ((r + t) % RING) * chunk + side * half + q]
    matrix = smoothing_matrix(total)
    matrix = jnp.concatenate(
        [lax.dynamic_slice_in_dim(matrix, s, q, axis=1) for s in starts], axis=1
    )
    outs = []
    for k in range(blocks.shape[0]):
        joined = jnp.concatenate([p[k] for p in pieces], axis=1)
        wide = jnp.broadcast_to(matrix, (joined.shape[0],) + matrix.shape)
        outs.append(jnp.einsum("xij,xjz->xiz", wide, joined, precision=HP))
    return outs


def smooth_depth(field):
    matrix = smoothing_matrix(field.shape[-1])
    return jnp.einsum("...j,ij->...i", field, matrix, precision=HP)


def smooth_along_x(both):
    cols = lax.all_to_all(both, "slab", split_axis=2, concat_axis=1, tiled=True)
    matrix = smoothing_matrix(cols.shape[1])
    cols = jnp.einsum("ij,fjyz->fiyz", matrix, cols, precision=HP)
    return lax.all_to_all(cols, "slab", split_axis=1, concat_axis=2, tiled=True)


def make_body(n_shots):
    def body(vel_parts, den_parts, illum_parts, layer_index, depth_scale):
        total = vel_parts.shape[2]
        illum, vel, den = reduce_scatter_shots(
            [illum_parts[0], vel_parts[0], den_parts[0]], n_shots
        )
        both = jnp.stack([vel / illum, den / illum])
        both = smooth_along_x(smooth_depth(both))
        vel, den = all_gather_smooth_shots(both, n_shots, total)
        onehot = (
            layer_index[:, None] == jnp.arange(depth_scale.shape[1], dtype=jnp.int32)[None, :]
        ).astype(jnp.float32)
        per_depth = jnp.dot(depth_scale, onehot.T, precision=HP)
        vel_update = per_depth[0][None, None, :] * vel
        den_update = per_depth[1][None, None, :] * den
        return (vel_update, den_update)

    return body


def solution(mesh):
    placed = (
        P("shots", "slab", None, None),
        P("shots", "slab", None, None),
        P("shots", "slab", None, None),
        P(),
        P(),
    )
    return jax.shard_map(
        make_body(mesh.shape["shots"]),
        mesh=mesh,
        in_specs=placed,
        out_specs=(P("slab", None, None), P("slab", None, None)),
        check_vma=False,
    )
```

```python
import jax
import jax.numpy as jnp
from jax import lax
from jax.sharding import PartitionSpec as P

RADIUS = 20
HP = lax.Precision.HIGHEST
RING = 4


def smoothing_matrix(count):
    cells = jnp.arange(count, dtype=jnp.int32)
    offset = (cells[:, None] - cells[None, :]).astype(jnp.float32)
    inside = jnp.abs(offset) <= RADIUS
    weights = jnp.where(inside, jnp.exp(-offset * offset / 200.0), jnp.float32(0.0))
    return weights / jnp.sum(weights, axis=1, keepdims=True)


def ring_pairs(n_shots, step):
    hi = n_shots // RING
    return [(h * RING + r, h * RING + (r + step) % RING) for h in range(hi) for r in range(RING)]


def hi_pairs(n_shots):
    hi = n_shots // RING
    return [(h * RING + r, ((h + 1) % hi) * RING + r) for h in range(hi) for r in range(RING)]


def rows(field, start, size):
    return lax.dynamic_slice_in_dim(field, start, size, axis=1)


def ring_sum(fields, starts, size, n_shots, gates=None):
    idx = lax.axis_index("shots")
    r = idx % RING
    q = size // 2
    fwd, bwd = ring_pairs(n_shots, 1), ring_pairs(n_shots, -1)

    def take(start):
        return jnp.stack([rows(f, start, q) for f in fields])

    acc_f = take(starts((r - 1) % RING))
    acc_b = take(starts((r + 1) % RING) + q)
    for t in range(1, RING):
        recv_f = lax.ppermute(acc_f, "shots", fwd)
        recv_b = lax.ppermute(acc_b, "shots", bwd)
        if gates is not None and t in gates:
            recv_f, recv_b, gates[t] = lax.optimization_barrier((recv_f, recv_b, gates[t]))
        acc_f = recv_f + take(starts((r - 1 - t) % RING))
        acc_b = recv_b + take(starts((r + 1 + t) % RING) + q)
    return jnp.concatenate([acc_f, acc_b], axis=2)


def reduce_scatter_shots(fields, n_shots):
    idx = lax.axis_index("shots")
    h = idx // RING
    chunk = fields[0].shape[1] // RING
    half = chunk // 2
    theirs = ring_sum(fields, lambda c: c * chunk + (1 - h) * half, half, n_shots)
    fields, theirs = lax.optimization_barrier((tuple(fields), theirs))
    q = half // 2
    gates = {
        RING - 2: lax.ppermute(theirs[:, :, :q], "shots", hi_pairs(n_shots)),
        RING - 1: lax.ppermute(theirs[:, :, q:], "shots", hi_pairs(n_shots)),
    }
    mine = ring_sum(fields, lambda c: c * chunk + h * half, half, n_shots, gates)
    return mine + jnp.concatenate([gates[RING - 2], gates[RING - 1]], axis=2)


def all_gather_smooth_shots(blocks, n_shots, total):
    idx = lax.axis_index("shots")
    r, h = idx % RING, idx // RING
    chunk = total // RING
    half = chunk // 2
    q = half // 2
    fwd, bwd = ring_pairs(n_shots, 1), ring_pairs(n_shots, -1)
    other_f = lax.ppermute(blocks[:, :, :q], "shots", hi_pairs(n_shots))
    rest, other_f = lax.optimization_barrier((blocks[:, :, q:], other_f))
    other_b = lax.ppermute(rest, "shots", hi_pairs(n_shots))
    pieces, starts = [], []
    for (cur_f, cur_b), side in (((blocks[:, :, :q], blocks[:, :, q:]), h), ((other_f, other_b), 1 - h)):
        pieces += [cur_f, cur_b]
        starts += [r * chunk + side * half, r * chunk + side * half + q]
        for t in range(1, RING):
            cur_f = lax.ppermute(cur_f, "shots", fwd)
            cur_b = lax.ppermute(cur_b, "shots", bwd)
            pieces += [cur_f, cur_b]
            starts += [((r - t) % RING) * chunk + side * half, ((r + t) % RING) * chunk + side * half + q]
    matrix = smoothing_matrix(total)
    matrix = jnp.concatenate(
        [lax.dynamic_slice_in_dim(matrix, s, q, axis=1) for s in starts], axis=1
    )
    outs = []
    for k in range(blocks.shape[0]):
        joined = jnp.concatenate([p[k] for p in pieces], axis=1)
        wide = jnp.broadcast_to(matrix, (joined.shape[0],) + matrix.shape)
        outs.append(jnp.einsum("xij,xjz->xiz", wide, joined, precision=HP))
    return outs


def smooth_depth(field):
    matrix = smoothing_matrix(field.shape[-1])
    return jnp.einsum("...j,ij->...i", field, matrix, precision=HP)


def smooth_along_x(both):
    cols = lax.all_to_all(both, "slab", split_axis=2, concat_axis=1, tiled=True)
    matrix = smoothing_matrix(cols.shape[1])
    cols = jnp.einsum("ij,fjyz->fiyz", matrix, cols, precision=HP)
    return lax.all_to_all(cols, "slab", split_axis=1, concat_axis=2, tiled=True)


def make_body(n_shots):
    def body(vel_parts, den_parts, illum_parts, layer_index, depth_scale):
        total = vel_parts.shape[2]
        illum, vel, den = reduce_scatter_shots(
            [illum_parts[0], vel_parts[0], den_parts[0]], n_shots
        )
        both = jnp.stack([vel / illum, den / illum])
        both = smooth_along_x(smooth_depth(both))
        vel, den = all_gather_smooth_shots(both, n_shots, total)
        onehot = (
            layer_index[:, None] == jnp.arange(depth_scale.shape[1], dtype=jnp.int32)[None, :]
        ).astype(jnp.float32)
        per_depth = jnp.dot(depth_scale, onehot.T, precision=HP)
        vel_update = per_depth[0][None, None, :] * vel
        den_update = per_depth[1][None, None, :] * den
        return (vel_update, den_update)

    return body


def solution(mesh):
    placed = (
        P("shots", "slab", None, None),
        P("shots", "slab", None, None),
        P("shots", "slab", None, None),
        P(),
        P(),
    )
    return jax.shard_map(
        make_body(mesh.shape["shots"]),
        mesh=mesh,
        in_specs=placed,
        out_specs=(P("slab", None, None), P("slab", None, None)),
        check_vma=False,
    )
```

```python
import jax
import jax.numpy as jnp
from jax import lax
from jax.sharding import PartitionSpec as P

RADIUS = 20
HP = lax.Precision.HIGHEST
RING = 4


def smoothing_matrix(count):
    cells = jnp.arange(count, dtype=jnp.int32)
    offset = (cells[:, None] - cells[None, :]).astype(jnp.float32)
    inside = jnp.abs(offset) <= RADIUS
    weights = jnp.where(inside, jnp.exp(-offset * offset / 200.0), jnp.float32(0.0))
    return weights / jnp.sum(weights, axis=1, keepdims=True)


def ring_pairs(n_shots, step):
    hi = n_shots // RING
    return [(h * RING + r, h * RING + (r + step) % RING) for h in range(hi) for r in range(RING)]


def hi_pairs(n_shots):
    hi = n_shots // RING
    return [(h * RING + r, ((h + 1) % hi) * RING + r) for h in range(hi) for r in range(RING)]


def rows(field, start, size):
    return lax.dynamic_slice_in_dim(field, start, size, axis=1)


def ring_sum(fields, starts, size, n_shots, gates=None):
    idx = lax.axis_index("shots")
    r = idx % RING
    q = size // 2
    fwd, bwd = ring_pairs(n_shots, 1), ring_pairs(n_shots, -1)

    def take(start):
        return jnp.stack([rows(f, start, q) for f in fields])

    acc_f = take(starts((r - 1) % RING))
    acc_b = take(starts((r + 1) % RING) + q)
    for t in range(1, RING):
        recv_f = lax.ppermute(acc_f, "shots", fwd)
        recv_b = lax.ppermute(acc_b, "shots", bwd)
        if gates is not None and t in gates:
            recv_f, recv_b, gates[t] = lax.optimization_barrier((recv_f, recv_b, gates[t]))
        acc_f = recv_f + take(starts((r - 1 - t) % RING))
        acc_b = recv_b + take(starts((r + 1 + t) % RING) + q)
    return jnp.concatenate([acc_f, acc_b], axis=2)


def reduce_scatter_shots(fields, n_shots):
    idx = lax.axis_index("shots")
    h = idx // RING
    chunk = fields[0].shape[1] // RING
    half = chunk // 2
    theirs = ring_sum(fields, lambda c: c * chunk + (1 - h) * half, half, n_shots)
    fields, theirs = lax.optimization_barrier((tuple(fields), theirs))
    cuts = [0, half // 4, half // 4 + 3 * half // 8, half]
    gates = {
        t: lax.ppermute(theirs[:, :, cuts[t - 1]:cuts[t]], "shots", hi_pairs(n_shots))
        for t in range(1, RING)
    }
    mine = ring_sum(fields, lambda c: c * chunk + h * half, half, n_shots, gates)
    return mine + jnp.concatenate([gates[t] for t in range(1, RING)], axis=2)


def all_gather_smooth_shots(blocks, n_shots, total):
    idx = lax.axis_index("shots")
    r, h = idx % RING, idx // RING
    chunk = total // RING
    half = chunk // 2
    q = half // 2
    fwd, bwd = ring_pairs(n_shots, 1), ring_pairs(n_shots, -1)
    other = lax.ppermute(blocks, "shots", hi_pairs(n_shots))
    pieces, starts = [], []
    for block, side in ((blocks, h), (other, 1 - h)):
        cur_f, cur_b = block[:, :, :q], block[:, :, q:]
        pieces += [cur_f, cur_b]
        starts += [r * chunk + side * half, r * chunk + side * half + q]
        for t in range(1, RING):
            cur_f = lax.ppermute(cur_f, "shots", fwd)
            cur_b = lax.ppermute(cur_b, "shots", bwd)
            pieces += [cur_f, cur_b]
            starts += [((r - t) % RING) * chunk + side * half, ((r + t) % RING) * chunk + side * half + q]
    matrix = smoothing_matrix(total)
    matrix = jnp.concatenate(
        [lax.dynamic_slice_in_dim(matrix, s, q, axis=1) for s in starts], axis=1
    )
    outs = []
    for k in range(blocks.shape[0]):
        joined = jnp.concatenate([p[k] for p in pieces], axis=1)
        wide = jnp.broadcast_to(matrix, (joined.shape[0],) + matrix.shape)
        outs.append(jnp.einsum("xij,xjz->xiz", wide, joined, precision=HP))
    return outs


def smooth_depth(field):
    matrix = smoothing_matrix(field.shape[-1])
    return jnp.einsum("...j,ij->...i", field, matrix, precision=HP)


def smooth_along_x(both):
    cols = lax.all_to_all(both, "slab", split_axis=2, concat_axis=1, tiled=True)
    matrix = smoothing_matrix(cols.shape[1])
    cols = jnp.einsum("ij,fjyz->fiyz", matrix, cols, precision=HP)
    return lax.all_to_all(cols, "slab", split_axis=1, concat_axis=2, tiled=True)


def make_body(n_shots):
    def body(vel_parts, den_parts, illum_parts, layer_index, depth_scale):
        total = vel_parts.shape[2]
        illum, vel, den = reduce_scatter_shots(
            [illum_parts[0], vel_parts[0], den_parts[0]], n_shots
        )
        both = jnp.stack([vel / illum, den / illum])
        both = smooth_along_x(smooth_depth(both))
        vel, den = all_gather_smooth_shots(both, n_shots, total)
        onehot = (
            layer_index[:, None] == jnp.arange(depth_scale.shape[1], dtype=jnp.int32)[None, :]
        ).astype(jnp.float32)
        per_depth = jnp.dot(depth_scale, onehot.T, precision=HP)
        vel_update = per_depth[0][None, None, :] * vel
        den_update = per_depth[1][None, None, :] * den
        return (vel_update, den_update)

    return body


def solution(mesh):
    placed = (
        P("shots", "slab", None, None),
        P("shots", "slab", None, None),
        P("shots", "slab", None, None),
        P(),
        P(),
    )
    return jax.shard_map(
        make_body(mesh.shape["shots"]),
        mesh=mesh,
        in_specs=placed,
        out_specs=(P("slab", None, None), P("slab", None, None)),
        check_vma=False,
    )
```
